128 devices in a mesh: gx: 8 (over y_hi, z), gy: 16 (over x, y_lo, core).
Axes of the slice: x: 4, y: 4 (y_hi: 2, y_lo: 2; y = y_hi * 2 + y_lo), z: 4, core: 2. Of those that a mesh axis runs over, the one named last changes fastest.
Arguments:
- observed: float32 [2, 8192, 8192], P(None, 'gx', 'gy'), may hold values from -6 to 6
- noise_var: float32 [8192, 8192], P('gx', 'gy'), may hold values from 0.05 to 0.5
- row_kernel: float32 [4096, 4096], P('gx'), may hold values from -1 to 1.2, as said below
- col_kernel: float32 [4096, 4096], P('gy'), may hold values from -1 to 1.2, as said below
Outputs:
- gram_times: float32 [2, 8192, 8192], P(None, 'gx', 'gy')
The draws below stay inside these ranges and needn't reach their ends.
Inputs may be any that keep to these rules, and one draw needn't show every extreme that they name: row_kernel is symmetric. col_kernel is symmetric.
All inputs are finite; a program needn't handle non-finite values.
Results may differ from the reference program's by a relative error of at most 0.000065.
Values sent between devices are 32-bit elements; how exact they have to be, the bound alone decides.
No kernel may reach another device: no remote copies, remote signals or barrier semaphores. Data moves between devices by JAX's collectives and lax.ppermute only.
A program may use at most 128 MiB of HBM per device.

```python
import math
import jax
import jax.numpy as jnp
from jax import lax

MX = 4096
MY = 4096
RHS = 2
NXO = 8192
NYO = 8192


def symmetric_kernel(key, order):
    base = jax.random.truncated_normal(key, -4.0, 4.0, (order, order), jnp.float32)
    offdiag = (base + base.T) * (0.3 / math.sqrt(2.0 * order))
    diagonal = jax.random.uniform(jax.random.fold_in(key, 7), (order,), jnp.float32, 0.8, 1.2)
    identity = jnp.eye(order, dtype=jnp.float32)
    return offdiag * (1.0 - identity) + identity * diagonal[None, :]


def draw_row_kernel(key, part):
    return symmetric_kernel(jax.random.fold_in(key, 11), MX)


def draw_col_kernel(key, part):
    return symmetric_kernel(jax.random.fold_in(key, 23), MY)


def shard_levels(key, shape, pieces, least, largest):
    def one(position, blocks):
        steps = jax.random.uniform(jax.random.fold_in(jax.random.fold_in(key, 6), position), (blocks,), jnp.float32, least / len(pieces), largest / len(pieces))
        return jnp.repeat(jnp.exp(steps), shape[position] // blocks).reshape((-1,) + (1,) * (len(shape) - position - 1))

    gain = one(*pieces[0])
    for cut in pieces[1:]:
        gain = gain * one(*cut)
    return gain


def gaussian(key, shape, scale, most, cuts=(), kind=jnp.bfloat16):
    gain = shard_levels(key, shape, cuts, -0.22, 0.18) if cuts else 1.0
    entries = jax.random.normal(key, shape, jnp.float32) * scale * gain
    return jnp.minimum(jnp.maximum(entries, -most), most).astype(kind)


def setup_inputs(seed: int = 0) -> dict:
    keys = jax.random.split(jax.random.key(seed), 5)
    return {
        "observed": gaussian(keys[0], (RHS, NXO, NYO), 1.0, 6.0, ((1, 8), (2, 16)), jnp.float32),
        "noise_var": jnp.clip(jnp.exp(math.log(0.5) - 2.3025851 * jax.random.uniform(keys[1], (NXO, NYO), jnp.float32) ** shard_levels(keys[1], (NXO, NYO), ((0, 8), (1, 16)), -0.2, 0.2)), 0.05, 0.5),
        "row_kernel": draw_row_kernel(jax.random.fold_in(keys[4], 71), 0),
        "col_kernel": draw_col_kernel(jax.random.fold_in(keys[4], 71), 0),
    }


even_taps = (-0.0703125, 0.8671875, 0.2265625, -0.0234375)
odd_taps = (-0.0234375, 0.2265625, 0.8671875, -0.0703125)


def adjoint_rows(extended, count):
    evens = extended[:, 0::2]
    odds = extended[:, 1::2]
    total = jnp.zeros((extended.shape[0], count, extended.shape[2]), jnp.float32)
    for index in range(4):
        start = 3 - index
        total = total + even_taps[index] * evens[:, start:start + count] + odd_taps[index] * odds[:, start:start + count]
    return total


def forward_rows(extended, count):
    first = jnp.zeros((extended.shape[0], count, extended.shape[2]), jnp.float32)
    second = jnp.zeros((extended.shape[0], count, extended.shape[2]), jnp.float32)
    for index in range(4):
        start = index + 1
        first = first + even_taps[index] * extended[:, start:start + count]
        second = second + odd_taps[index] * extended[:, start:start + count]
    stacked = jnp.stack([first, second], axis=2)
    return stacked.reshape(extended.shape[0], 2 * count, extended.shape[2])


def swap_last(field):
    return jnp.transpose(field, (0, 2, 1))


def reference(observed, noise_var, row_kernel, col_kernel):
    padded = jnp.pad(observed, ((0, 0), (4, 4), (0, 0)))
    rowsum = adjoint_rows(padded, MX)
    padded = jnp.pad(swap_last(rowsum), ((0, 0), (4, 4), (0, 0)))
    inducing = swap_last(adjoint_rows(padded, MY))
    mixed = jnp.einsum("rik,jk->rij", inducing, col_kernel, precision=lax.Precision.HIGHEST)
    product = jnp.einsum("ik,rkj->rij", row_kernel, mixed, precision=lax.Precision.HIGHEST)
    padded = jnp.pad(swap_last(product), ((0, 0), (2, 2), (0, 0)))
    colpass = swap_last(forward_rows(padded, MY))
    padded = jnp.pad(colpass, ((0, 0), (2, 2), (0, 0)))
    result = forward_rows(padded, MX)
    return result + noise_var[None] * observed
```

```python
import jax
import jax.numpy as jnp
from jax import lax
from jax.sharding import PartitionSpec as P


def with_halo(cells, sides, width):
    for axis, dim in sides:
        count = lax.axis_size(axis)
        ends = count - 1
        head = lax.slice_in_dim(cells, 0, width, axis=dim)
        tail = lax.slice_in_dim(cells, cells.shape[dim] - width, cells.shape[dim], axis=dim)
        cells = jnp.concatenate(
            [
                lax.ppermute(tail, axis, [(i, (i + 1) % count) for i in range(ends)]),
                cells,
                lax.ppermute(head, axis, [((i + 1) % count, i) for i in range(ends)]),
            ],
            axis=dim,
        )
    return cells


def keys_weight(dist):
    span = jnp.abs(dist)
    inner = (1.5 * span - 2.5) * span * span + 1.0
    outer = ((-0.5 * span + 2.5) * span - 4.0) * span + 2.0
    return jnp.where(span < 1.0, inner, jnp.where(span < 2.0, outer, 0.0))


def tap_table(rows, cols, coarse_on_rows, pad):
    r = lax.broadcasted_iota(jnp.float32, (rows, cols), 0)
    c = lax.broadcasted_iota(jnp.float32, (rows, cols), 1)
    if coarse_on_rows:
        coarse, fine = r, c
    else:
        coarse, fine = c, r
    if pad == 4:
        dist = coarse - ((fine - 4.0) * 0.5 + 0.25)
    else:
        dist = coarse - 2.0 - (fine * 0.5 + 0.25)
    return keys_weight(dist).astype(jnp.bfloat16)


def split3(x):
    hi = lax.reduce_precision(x, exponent_bits=8, mantissa_bits=7)
    rest = x - hi
    mid = lax.reduce_precision(rest, exponent_bits=8, mantissa_bits=7)
    lo = rest - mid
    return hi.astype(jnp.bfloat16), mid.astype(jnp.bfloat16), lo.astype(jnp.bfloat16)


def exact_dot(eq, x, table, data_first):
    total = None
    for part in split3(x):
        if data_first:
            term = jnp.einsum(eq, part, table, preferred_element_type=jnp.float32)
        else:
            term = jnp.einsum(eq, table, part, preferred_element_type=jnp.float32)
        total = term if total is None else total + term
    return total


def body(observed, noise_var, row_kernel, col_kernel):
    highest = lax.Precision.HIGHEST
    tile_rows = row_kernel.shape[0]
    tile_cols = col_kernel.shape[0]
    extended = with_halo(observed, (("gx", 1), ("gy", 2)), 4)
    col_adj = tap_table(2 * tile_cols + 8, tile_cols, False, 4)
    row_adj = tap_table(tile_rows, 2 * tile_rows + 8, True, 4)
    colsum = exact_dot("rpq,qj->rpj", extended, col_adj, True)
    inducing = exact_dot("ip,rpj->rij", colsum, row_adj, False)
    mixed = jnp.einsum(
        "rik,jk->rij", lax.all_gather(inducing, "gy", axis=2, tiled=True), col_kernel, precision=highest
    )
    product = jnp.einsum(
        "ik,rkj->rij", row_kernel, lax.all_gather(mixed, "gx", axis=1, tiled=True), precision=highest
    )
    coarse_ext = with_halo(product, (("gx", 1), ("gy", 2)), 2)
    row_fwd = tap_table(2 * tile_rows, tile_rows + 4, False, 2)
    col_fwd = tap_table(tile_cols + 4, 2 * tile_cols, True, 2)
    rowpass = exact_dot("pi,rij->rpj", coarse_ext, row_fwd, False)
    result = exact_dot("rpj,jq->rpq", rowpass, col_fwd, True)
    return result + noise_var[None] * observed


def solution(mesh):
    return jax.shard_map(
        body,
        mesh=mesh,
        in_specs=(P(None, "gx", "gy"), P("gx", "gy"), P("gx", None), P("gy", None)),
        out_specs=P(None, "gx", "gy"),
        check_vma=False,
    )
```

```python
import jax
import jax.numpy as jnp
from jax import lax
from jax.sharding import Mesh, PartitionSpec as P


def axis_count(axis):
    return lax.psum(1, axis)


def with_halo(cells, sides, width):
    for axis, dim in sides:
        count = axis_count(axis)
        ends = count - 1
        head = lax.slice_in_dim(cells, 0, width, axis=dim)
        tail = lax.slice_in_dim(cells, cells.shape[dim] - width, cells.shape[dim], axis=dim)
        cells = jnp.concatenate(
            [
                lax.ppermute(tail, axis, [(i, (i + 1) % count) for i in range(ends)]),
                cells,
                lax.ppermute(head, axis, [((i + 1) % count, i) for i in range(ends)]),
            ],
            axis=dim,
        )
    return cells


def keys_weight(dist):
    span = jnp.abs(dist)
    inner = (1.5 * span - 2.5) * span * span + 1.0
    outer = ((-0.5 * span + 2.5) * span - 4.0) * span + 2.0
    return jnp.where(span < 1.0, inner, jnp.where(span < 2.0, outer, 0.0))


def tap_table(rows, cols, coarse_on_rows, pad):
    r = lax.broadcasted_iota(jnp.float32, (rows, cols), 0)
    c = lax.broadcasted_iota(jnp.float32, (rows, cols), 1)
    if coarse_on_rows:
        coarse, fine = r, c
    else:
        coarse, fine = c, r
    if pad == 4:
        dist = coarse - ((fine - 4.0) * 0.5 + 0.25)
    else:
        dist = coarse - 2.0 - (fine * 0.5 + 0.25)
    return keys_weight(dist).astype(jnp.bfloat16)


def split3(x):
    hi = lax.reduce_precision(x, exponent_bits=8, mantissa_bits=7)
    rest = x - hi
    mid = lax.reduce_precision(rest, exponent_bits=8, mantissa_bits=7)
    lo = rest - mid
    return hi.astype(jnp.bfloat16), mid.astype(jnp.bfloat16), lo.astype(jnp.bfloat16)


def exact_dot(eq, x, table, data_first):
    total = None
    for part in split3(x):
        if data_first:
            term = jnp.einsum(eq, part, table, preferred_element_type=jnp.float32)
        else:
            term = jnp.einsum(eq, table, part, preferred_element_type=jnp.float32)
        total = term if total is None else total + term
    return total


def body(observed, noise_var, row_kernel, col_kernel):
    highest = lax.Precision.HIGHEST
    rows_axis = ("yh", "z")
    cols_axis = ("x", "yl", "core")
    tile_rows = row_kernel.shape[0]
    tile_cols = col_kernel.shape[0]
    core = lax.axis_index("core")
    swap = [(0, 1), (1, 0)]
    by_parity = col_kernel.reshape(tile_cols, -1, 2, tile_cols)
    own_part = lax.dynamic_index_in_dim(by_parity, core, axis=2, keepdims=False)
    other_part = lax.dynamic_index_in_dim(by_parity, 1 - core, axis=2, keepdims=False)
    partner_part = lax.ppermute(other_part, "core", swap)
    extended = with_halo(observed, ((rows_axis, 1), (cols_axis, 2)), 4)
    col_adj = tap_table(2 * tile_cols + 8, tile_cols, False, 4)
    row_adj = tap_table(tile_rows, 2 * tile_rows + 8, True, 4)
    colsum = exact_dot("rpq,qj->rpj", extended, col_adj, True)
    inducing = exact_dot("ip,rpj->rij", colsum, row_adj, False)
    gathered = lax.all_gather(inducing, ("x", "yl"), axis=2, tiled=True)
    own_sum = jnp.einsum(
        "rik,jk->rij", gathered, own_part.reshape(tile_cols, -1), precision=highest
    )
    partner_sum = jnp.einsum(
        "rik,jk->rij", gathered, partner_part.reshape(tile_cols, -1), precision=highest
    )
    mixed = own_sum + lax.ppermute(partner_sum, "core", swap)
    product = jnp.einsum(
        "ik,rkj->rij", row_kernel, lax.all_gather(mixed, rows_axis, axis=1, tiled=True), precision=highest
    )
    coarse_ext = with_halo(product, ((rows_axis, 1), (cols_axis, 2)), 2)
    row_fwd = tap_table(2 * tile_rows, tile_rows + 4, False, 2)
    col_fwd = tap_table(tile_cols + 4, 2 * tile_cols, True, 2)
    rowpass = exact_dot("pi,rij->rpj", coarse_ext, row_fwd, False)
    result = exact_dot("rpj,jq->rpq", rowpass, col_fwd, True)
    return result + noise_var[None] * observed


def solution(mesh):
    rows_n, cols_n = mesh.devices.shape
    z = min(4, rows_n)
    shape = (rows_n // z, z, cols_n // 4, 2, 2)
    fine = Mesh(mesh.devices.reshape(shape), ("yh", "z", "x", "yl", "core"))
    rows = ("yh", "z")
    cols = ("x", "yl", "core")
    return jax.shard_map(
        body,
        mesh=fine,
        in_specs=(P(None, rows, cols), P(rows, cols), P(rows, None), P(cols, None)),
        out_specs=P(None, rows, cols),
        check_vma=False,
    )
```

```python
import jax
import jax.numpy as jnp
from jax import lax
from jax.sharding import PartitionSpec as P


def with_halo(cells, sides, width):
    for axis, dim in sides:
        count = lax.axis_size(axis)
        ends = count - 1
        head = lax.slice_in_dim(cells, 0, width, axis=dim)
        tail = lax.slice_in_dim(cells, cells.shape[dim] - width, cells.shape[dim], axis=dim)
        cells = jnp.concatenate(
            [
                lax.ppermute(tail, axis, [(i, (i + 1) % count) for i in range(ends)]),
                cells,
                lax.ppermute(head, axis, [((i + 1) % count, i) for i in range(ends)]),
            ],
            axis=dim,
        )
    return cells


def keys_weight(dist):
    span = jnp.abs(dist)
    inner = (1.5 * span - 2.5) * span * span + 1.0
    outer = ((-0.5 * span + 2.5) * span - 4.0) * span + 2.0
    return jnp.where(span < 1.0, inner, jnp.where(span < 2.0, outer, 0.0))


def tap_table(rows, cols, coarse_on_rows, pad):
    r = lax.broadcasted_iota(jnp.float32, (rows, cols), 0)
    c = lax.broadcasted_iota(jnp.float32, (rows, cols), 1)
    if coarse_on_rows:
        coarse, fine = r, c
    else:
        coarse, fine = c, r
    if pad == 4:
        dist = coarse - ((fine - 4.0) * 0.5 + 0.25)
    else:
        dist = coarse - 2.0 - (fine * 0.5 + 0.25)
    return keys_weight(dist).astype(jnp.bfloat16)


def split3(x):
    hi = lax.reduce_precision(x, exponent_bits=8, mantissa_bits=7)
    rest = x - hi
    mid = lax.reduce_precision(rest, exponent_bits=8, mantissa_bits=7)
    lo = rest - mid
    return hi.astype(jnp.bfloat16), mid.astype(jnp.bfloat16), lo.astype(jnp.bfloat16)


def exact_dot(eq, x, table, data_first):
    total = None
    for part in split3(x):
        if data_first:
            term = jnp.einsum(eq, part, table, preferred_element_type=jnp.float32)
        else:
            term = jnp.einsum(eq, table, part, preferred_element_type=jnp.float32)
        total = term if total is None else total + term
    return total


def body(observed, noise_var, row_kernel, col_kernel):
    highest = lax.Precision.HIGHEST
    tile_rows = row_kernel.shape[0]
    tile_cols = col_kernel.shape[0]
    extended = with_halo(observed, (("gx", 1), ("gy", 2)), 4)
    col_adj = tap_table(2 * tile_cols + 8, tile_cols, False, 4)
    row_adj = tap_table(tile_rows, 2 * tile_rows + 8, True, 4)
    row_fwd = tap_table(2 * tile_rows, tile_rows + 4, False, 2)
    col_fwd = tap_table(tile_cols + 4, 2 * tile_cols, True, 2)
    results = []
    for side in range(observed.shape[0]):
        cells = extended[side : side + 1]
        colsum = exact_dot("rpq,qj->rpj", cells, col_adj, True)
        inducing = exact_dot("ip,rpj->rij", colsum, row_adj, False)
        mixed = jnp.einsum(
            "rik,jk->rij", lax.all_gather(inducing, "gy", axis=2, tiled=True), col_kernel, precision=highest
        )
        product = jnp.einsum(
            "ik,rkj->rij", row_kernel, lax.all_gather(mixed, "gx", axis=1, tiled=True), precision=highest
        )
        coarse_ext = with_halo(product, (("gx", 1), ("gy", 2)), 2)
        rowpass = exact_dot("pi,rij->rpj", coarse_ext, row_fwd, False)
        results.append(exact_dot("rpj,jq->rpq", rowpass, col_fwd, True))
    return jnp.concatenate(results, axis=0) + noise_var[None] * observed


def solution(mesh):
    return jax.shard_map(
        body,
        mesh=mesh,
        in_specs=(P(None, "gx", "gy"), P("gx", "gy"), P("gx", None), P("gy", None)),
        out_specs=P(None, "gx", "gy"),
        check_vma=False,
    )
```

```python
import jax
import jax.numpy as jnp
from jax import lax
from jax.sharding import PartitionSpec as P


def with_halo(cells, sides, width):
    for axis, dim in sides:
        count = lax.axis_size(axis)
        ends = count - 1
        head = lax.slice_in_dim(cells, 0, width, axis=dim)
        tail = lax.slice_in_dim(cells, cells.shape[dim] - width, cells.shape[dim], axis=dim)
        cells = jnp.concatenate(
            [
                lax.ppermute(tail, axis, [(i, (i + 1) % count) for i in range(ends)]),
                cells,
                lax.ppermute(head, axis, [((i + 1) % count, i) for i in range(ends)]),
            ],
            axis=dim,
        )
    return cells


def keys_weight(dist):
    span = jnp.abs(dist)
    inner = (1.5 * span - 2.5) * span * span + 1.0
    outer = ((-0.5 * span + 2.5) * span - 4.0) * span + 2.0
    return jnp.where(span < 1.0, inner, jnp.where(span < 2.0, outer, 0.0))


def tap_table(rows, cols, coarse_on_rows, pad):
    r = lax.broadcasted_iota(jnp.float32, (rows, cols), 0)
    c = lax.broadcasted_iota(jnp.float32, (rows, cols), 1)
    if coarse_on_rows:
        coarse, fine = r, c
    else:
        coarse, fine = c, r
    if pad == 4:
        dist = coarse - ((fine - 4.0) * 0.5 + 0.25)
    else:
        dist = coarse - 2.0 - (fine * 0.5 + 0.25)
    return keys_weight(dist).astype(jnp.bfloat16)


def split3(x):
    hi = lax.reduce_precision(x, exponent_bits=8, mantissa_bits=7)
    rest = x - hi
    mid = lax.reduce_precision(rest, exponent_bits=8, mantissa_bits=7)
    lo = rest - mid
    return hi.astype(jnp.bfloat16), mid.astype(jnp.bfloat16), lo.astype(jnp.bfloat16)


def exact_dot(eq, x, table, data_first):
    total = None
    for part in split3(x):
        if data_first:
            term = jnp.einsum(eq, part, table, preferred_element_type=jnp.float32)
        else:
            term = jnp.einsum(eq, table, part, preferred_element_type=jnp.float32)
        total = term if total is None else total + term
    return total


def windows(kernel, starts, width):
    padded = jnp.pad(kernel, ((0, 0), (2, 2)))
    return jnp.concatenate([padded[:, start : start + width] for start in starts], axis=1)


def body(observed, noise_var, row_kernel, col_kernel):
    highest = lax.Precision.HIGHEST
    tile_rows = row_kernel.shape[0]
    tile_cols = col_kernel.shape[0]
    ext_rows = tile_rows + 4
    ext_cols = tile_cols + 4
    row_count = lax.axis_size("gx")
    col_count = lax.axis_size("gy")
    col_rows = with_halo(col_kernel, (("gy", 0),), 2)
    row_rows = with_halo(row_kernel, (("gx", 0),), 2)
    col_big = windows(col_rows, [tile_cols * c for c in range(col_count)], ext_cols)
    row_big = windows(row_rows, [tile_rows * c for c in range(row_count)], ext_rows)
    col_adj = tap_table(2 * tile_cols, ext_cols, False, 2)
    row_adj = tap_table(ext_rows, 2 * tile_rows, True, 2)
    colsum = exact_dot("rpq,qj->rpj", observed, col_adj, True)
    inducing = exact_dot("ip,rpj->rij", colsum, row_adj, False)
    mixed = jnp.einsum(
        "rik,jk->rij", lax.all_gather(inducing, "gy", axis=2, tiled=True), col_big, precision=highest
    )
    product = jnp.einsum(
        "ik,rkj->rij", row_big, lax.all_gather(mixed, "gx", axis=1, tiled=True), precision=highest
    )
    row_fwd = tap_table(2 * tile_rows, ext_rows, False, 2)
    col_fwd = tap_table(ext_cols, 2 * tile_cols, True, 2)
    rowpass = exact_dot("pi,rij->rpj", product, row_fwd, False)
    result = exact_dot("rpj,jq->rpq", rowpass, col_fwd, True)
    return result + noise_var[None] * observed


def solution(mesh):
    return jax.shard_map(
        body,
        mesh=mesh,
        in_specs=(P(None, "gx", "gy"), P("gx", "gy"), P("gx", None), P("gy", None)),
        out_specs=P(None, "gx", "gy"),
        check_vma=False,
    )
```

```python
import jax
import jax.numpy as jnp
from jax import lax
from jax.sharding import PartitionSpec as P


def with_halo(cells, sides, width):
    for axis, dim in sides:
        count = lax.axis_size(axis)
        ends = count - 1
        head = lax.slice_in_dim(cells, 0, width, axis=dim)
        tail = lax.slice_in_dim(cells, cells.shape[dim] - width, cells.shape[dim], axis=dim)
        cells = jnp.concatenate(
            [
                lax.ppermute(tail, axis, [(i, (i + 1) % count) for i in range(ends)]),
                cells,
                lax.ppermute(head, axis, [((i + 1) % count, i) for i in range(ends)]),
            ],
            axis=dim,
        )
    return cells


def keys_weight(dist):
    span = jnp.abs(dist)
    inner = (1.5 * span - 2.5) * span * span + 1.0
    outer = ((-0.5 * span + 2.5) * span - 4.0) * span + 2.0
    return jnp.where(span < 1.0, inner, jnp.where(span < 2.0, outer, 0.0))


def tap_table(rows, cols, coarse_on_rows, pad):
    r = lax.broadcasted_iota(jnp.float32, (rows, cols), 0)
    c = lax.broadcasted_iota(jnp.float32, (rows, cols), 1)
    if coarse_on_rows:
        coarse, fine = r, c
    else:
        coarse, fine = c, r
    if pad == 4:
        dist = coarse - ((fine - 4.0) * 0.5 + 0.25)
    else:
        dist = coarse - 2.0 - (fine * 0.5 + 0.25)
    return keys_weight(dist).astype(jnp.bfloat16)


def split3(x):
    hi = lax.reduce_precision(x, exponent_bits=8, mantissa_bits=7)
    rest = x - hi
    mid = lax.reduce_precision(rest, exponent_bits=8, mantissa_bits=7)
    lo = rest - mid
    return hi.astype(jnp.bfloat16), mid.astype(jnp.bfloat16), lo.astype(jnp.bfloat16)


def exact_dot(eq, x, table, data_first):
    total = None
    for part in split3(x):
        if data_first:
            term = jnp.einsum(eq, part, table, preferred_element_type=jnp.float32)
        else:
            term = jnp.einsum(eq, table, part, preferred_element_type=jnp.float32)
        total = term if total is None else total + term
    return total


def row_windows(kernel, count, block, width):
    padded = jnp.pad(kernel, ((0, width - kernel.shape[0]), (2, width - block - 2)))
    return jnp.concatenate([padded[:, block * w : block * w + width] for w in range(count)], axis=1)


def body(observed, noise_var, row_kernel, col_kernel):
    highest = lax.Precision.HIGHEST
    tile_rows = row_kernel.shape[0]
    tile_cols = col_kernel.shape[0]
    ext_rows = tile_rows + 8
    row_count = lax.axis_size("gx")
    row_rows = with_halo(row_kernel, (("gx", 0),), 2)
    row_big = row_windows(row_rows, row_count, tile_rows, ext_rows)
    extended = with_halo(observed, (("gy", 2),), 4)
    col_adj = tap_table(2 * tile_cols + 8, tile_cols, False, 4)
    row_adj = tap_table(ext_rows, 2 * tile_rows, True, 2)
    colsum = exact_dot("rpq,qj->rpj", extended, col_adj, True)
    inducing = exact_dot("ip,rpj->rij", colsum, row_adj, False)
    mixed = jnp.einsum(
        "rik,jk->rij", lax.all_gather(inducing, "gy", axis=2, tiled=True), col_kernel, precision=highest
    )
    product = jnp.einsum(
        "ik,rkj->rij", row_big, lax.all_gather(mixed, "gx", axis=1, tiled=True), precision=highest
    )
    coarse_ext = with_halo(product, (("gy", 2),), 2)
    row_fwd = tap_table(2 * tile_rows, ext_rows, False, 2)
    col_fwd = tap_table(tile_cols + 4, 2 * tile_cols, True, 2)
    rowpass = exact_dot("pi,rij->rpj", coarse_ext, row_fwd, False)
    result = exact_dot("rpj,jq->rpq", rowpass, col_fwd, True)
    return result + noise_var[None] * observed


def solution(mesh):
    return jax.shard_map(
        body,
        mesh=mesh,
        in_specs=(P(None, "gx", "gy"), P("gx", "gy"), P("gx", None), P("gy", None)),
        out_specs=P(None, "gx", "gy"),
        check_vma=False,
    )
```

```python
import jax
import jax.numpy as jnp
from jax import lax
from jax.sharding import PartitionSpec as P


def with_halo(cells, sides, width):
    for axis, dim in sides:
        count = lax.axis_size(axis)
        ends = count - 1
        head = lax.slice_in_dim(cells, 0, width, axis=dim)
        tail = lax.slice_in_dim(cells, cells.shape[dim] - width, cells.shape[dim], axis=dim)
        cells = jnp.concatenate(
            [
                lax.ppermute(tail, axis, [(i, (i + 1) % count) for i in range(ends)]),
                cells,
                lax.ppermute(head, axis, [((i + 1) % count, i) for i in range(ends)]),
            ],
            axis=dim,
        )
    return cells


def keys_weight(dist):
    span = jnp.abs(dist)
    inner = (1.5 * span - 2.5) * span * span + 1.0
    outer = ((-0.5 * span + 2.5) * span - 4.0) * span + 2.0
    return jnp.where(span < 1.0, inner, jnp.where(span < 2.0, outer, 0.0))


def tap_table(rows, cols, coarse_on_rows, pad):
    r = lax.broadcasted_iota(jnp.float32, (rows, cols), 0)
    c = lax.broadcasted_iota(jnp.float32, (rows, cols), 1)
    if coarse_on_rows:
        coarse, fine = r, c
    else:
        coarse, fine = c, r
    if pad == 4:
        dist = coarse - ((fine - 4.0) * 0.5 + 0.25)
    else:
        dist = coarse - 2.0 - (fine * 0.5 + 0.25)
    return keys_weight(dist).astype(jnp.bfloat16)


def split3(x):
    hi = lax.reduce_precision(x, exponent_bits=8, mantissa_bits=7)
    rest = x - hi
    mid = lax.reduce_precision(rest, exponent_bits=8, mantissa_bits=7)
    lo = rest - mid
    return hi.astype(jnp.bfloat16), mid.astype(jnp.bfloat16), lo.astype(jnp.bfloat16)


def exact_dot(eq, x, table, data_first):
    total = None
    for part in split3(x):
        if data_first:
            term = jnp.einsum(eq, part, table, preferred_element_type=jnp.float32)
        else:
            term = jnp.einsum(eq, table, part, preferred_element_type=jnp.float32)
        total = term if total is None else total + term
    return total


def row_windows(kernel, count, block, width):
    padded = jnp.pad(kernel, ((0, width - kernel.shape[0]), (2, width - block - 2)))
    return jnp.concatenate([padded[:, block * w : block * w + width] for w in range(count)], axis=1)


def body(observed, noise_var, row_kernel, col_kernel):
    highest = lax.Precision.HIGH
    tile_rows = row_kernel.shape[0]
    tile_cols = col_kernel.shape[0]
    ext_rows = tile_rows + 8
    row_count = lax.axis_size("gx")
    row_rows = with_halo(row_kernel, (("gx", 0),), 2)
    row_big = row_windows(row_rows, row_count, tile_rows, ext_rows)
    extended = with_halo(observed, (("gy", 2),), 4)
    col_adj = tap_table(2 * tile_cols + 8, tile_cols, False, 4)
    row_adj = tap_table(ext_rows, 2 * tile_rows, True, 2)
    colsum = exact_dot("rpq,qj->rpj", extended, col_adj, True)
    inducing = exact_dot("ip,rpj->rij", colsum, row_adj, False)
    mixed = jnp.einsum(
        "rik,jk->rij", lax.all_gather(inducing, "gy", axis=2, tiled=True), col_kernel, precision=highest
    )
    product = jnp.einsum(
        "ik,rkj->rij", row_big, lax.all_gather(mixed, "gx", axis=1, tiled=True), precision=highest
    )
    coarse_ext = with_halo(product, (("gy", 2),), 2)
    row_fwd = tap_table(2 * tile_rows, ext_rows, False, 2)
    col_fwd = tap_table(tile_cols + 4, 2 * tile_cols, True, 2)
    rowpass = exact_dot("pi,rij->rpj", coarse_ext, row_fwd, False)
    result = exact_dot("rpj,jq->rpq", rowpass, col_fwd, True)
    return result + noise_var[None] * observed


def solution(mesh):
    return jax.shard_map(
        body,
        mesh=mesh,
        in_specs=(P(None, "gx", "gy"), P("gx", "gy"), P("gx", None), P("gy", None)),
        out_specs=P(None, "gx", "gy"),
        check_vma=False,
    )
```

```python
import jax
import jax.numpy as jnp
from jax import lax
from jax.sharding import Mesh, PartitionSpec as P


def axis_count(axis):
    return lax.psum(1, axis)


def with_halo(cells, sides, width):
    for axis, dim in sides:
        count = axis_count(axis)
        ends = count - 1
        head = lax.slice_in_dim(cells, 0, width, axis=dim)
        tail = lax.slice_in_dim(cells, cells.shape[dim] - width, cells.shape[dim], axis=dim)
        cells = jnp.concatenate(
            [
                lax.ppermute(tail, axis, [(i, (i + 1) % count) for i in range(ends)]),
                cells,
                lax.ppermute(head, axis, [((i + 1) % count, i) for i in range(ends)]),
            ],
            axis=dim,
        )
    return cells


def keys_weight(dist):
    span = jnp.abs(dist)
    inner = (1.5 * span - 2.5) * span * span + 1.0
    outer = ((-0.5 * span + 2.5) * span - 4.0) * span + 2.0
    return jnp.where(span < 1.0, inner, jnp.where(span < 2.0, outer, 0.0))


def tap_table(rows, cols, coarse_on_rows, pad):
    r = lax.broadcasted_iota(jnp.float32, (rows, cols), 0)
    c = lax.broadcasted_iota(jnp.float32, (rows, cols), 1)
    if coarse_on_rows:
        coarse, fine = r, c
    else:
        coarse, fine = c, r
    if pad == 4:
        dist = coarse - ((fine - 4.0) * 0.5 + 0.25)
    else:
        dist = coarse - 2.0 - (fine * 0.5 + 0.25)
    return keys_weight(dist).astype(jnp.bfloat16)


def split3(x):
    hi = lax.reduce_precision(x, exponent_bits=8, mantissa_bits=7)
    rest = x - hi
    mid = lax.reduce_precision(rest, exponent_bits=8, mantissa_bits=7)
    lo = rest - mid
    return hi.astype(jnp.bfloat16), mid.astype(jnp.bfloat16), lo.astype(jnp.bfloat16)


def exact_dot(eq, x, table, data_first):
    total = None
    for part in split3(x):
        if data_first:
            term = jnp.einsum(eq, part, table, preferred_element_type=jnp.float32)
        else:
            term = jnp.einsum(eq, table, part, preferred_element_type=jnp.float32)
        total = term if total is None else total + term
    return total


def row_windows(kernel, count, block, width):
    padded = jnp.pad(kernel, ((0, width - kernel.shape[0]), (2, width - block - 2)))
    return jnp.concatenate([padded[:, block * w : block * w + width] for w in range(count)], axis=1)


def body(observed, noise_var, row_kernel, col_kernel):
    highest = lax.Precision.HIGH
    rows_axis = ("yh", "z")
    cols_axis = ("x", "yl", "core")
    tile_rows = row_kernel.shape[0]
    tile_cols = col_kernel.shape[0]
    ext_rows = tile_rows + 8
    row_count = axis_count(rows_axis)
    swap = [(0, 1), (1, 0)]
    side = lax.axis_index("yl")
    halves = col_kernel.reshape(tile_cols, -1, 2, 2 * tile_cols)
    near_cols = lax.dynamic_index_in_dim(halves, side, axis=2, keepdims=False).reshape(tile_cols, -1)
    far_cols = lax.dynamic_index_in_dim(halves, 1 - side, axis=2, keepdims=False).reshape(tile_cols, -1)
    partner_cols = lax.ppermute(far_cols, "yl", swap)
    row_rows = with_halo(row_kernel, ((rows_axis, 0),), 2)
    row_big = row_windows(row_rows, row_count, tile_rows, ext_rows)
    extended = with_halo(observed, ((cols_axis, 2),), 4)
    col_adj = tap_table(2 * tile_cols + 8, tile_cols, False, 4)
    row_adj = tap_table(ext_rows, 2 * tile_rows, True, 2)
    colsum = exact_dot("rpq,qj->rpj", extended, col_adj, True)
    inducing = exact_dot("ip,rpj->rij", colsum, row_adj, False)
    half = lax.all_gather(inducing, ("x", "core"), axis=2, tiled=True)
    near = jnp.einsum("rik,jk->rij", half, near_cols, precision=highest)
    for_partner = jnp.einsum("rik,jk->rij", half, partner_cols, precision=highest)
    mixed = near + lax.ppermute(for_partner, "yl", swap)
    product = jnp.einsum(
        "ik,rkj->rij", row_big, lax.all_gather(mixed, rows_axis, axis=1, tiled=True), precision=highest
    )
    coarse_ext = with_halo(product, ((cols_axis, 2),), 2)
    row_fwd = tap_table(2 * tile_rows, ext_rows, False, 2)
    col_fwd = tap_table(tile_cols + 4, 2 * tile_cols, True, 2)
    rowpass = exact_dot("pi,rij->rpj", coarse_ext, row_fwd, False)
    result = exact_dot("rpj,jq->rpq", rowpass, col_fwd, True)
    return result + noise_var[None] * observed


def solution(mesh):
    rows_n, cols_n = mesh.devices.shape
    z = min(4, rows_n)
    shape = (rows_n // z, z, cols_n // 4, 2, 2)
    fine = Mesh(mesh.devices.reshape(shape), ("yh", "z", "x", "yl", "core"))
    rows = ("yh", "z")
    cols = ("x", "yl", "core")
    return jax.shard_map(
        body,
        mesh=fine,
        in_specs=(P(None, rows, cols), P(rows, cols), P(rows, None), P(cols, None)),
        out_specs=P(None, rows, cols),
        check_vma=False,
    )
```

```python
import jax
import jax.numpy as jnp
from jax import lax
from jax.sharding import Mesh, PartitionSpec as P


def axis_count(axis):
    return lax.psum(1, axis)


def with_halo(cells, sides, width):
    for axis, dim in sides:
        count = axis_count(axis)
        ends = count - 1
        head = lax.slice_in_dim(cells, 0, width, axis=dim)
        tail = lax.slice_in_dim(cells, cells.shape[dim] - width, cells.shape[dim], axis=dim)
        cells = jnp.concatenate(
            [
                lax.ppermute(tail, axis, [(i, (i + 1) % count) for i in range(ends)]),
                cells,
                lax.ppermute(head, axis, [((i + 1) % count, i) for i in range(ends)]),
            ],
            axis=dim,
        )
    return cells


def keys_weight(dist):
    span = jnp.abs(dist)
    inner = (1.5 * span - 2.5) * span * span + 1.0
    outer = ((-0.5 * span + 2.5) * span - 4.0) * span + 2.0
    return jnp.where(span < 1.0, inner, jnp.where(span < 2.0, outer, 0.0))


def tap_table(rows, cols, coarse_on_rows, pad):
    r = lax.broadcasted_iota(jnp.float32, (rows, cols), 0)
    c = lax.broadcasted_iota(jnp.float32, (rows, cols), 1)
    if coarse_on_rows:
        coarse, fine = r, c
    else:
        coarse, fine = c, r
    if pad == 4:
        dist = coarse - ((fine - 4.0) * 0.5 + 0.25)
    else:
        dist = coarse - 2.0 - (fine * 0.5 + 0.25)
    return keys_weight(dist).astype(jnp.bfloat16)


def split3(x):
    hi = lax.reduce_precision(x, exponent_bits=8, mantissa_bits=7)
    rest = x - hi
    mid = lax.reduce_precision(rest, exponent_bits=8, mantissa_bits=7)
    lo = rest - mid
    return hi.astype(jnp.bfloat16), mid.astype(jnp.bfloat16), lo.astype(jnp.bfloat16)


def exact_dot(eq, x, table, data_first):
    total = None
    for part in split3(x):
        if data_first:
            term = jnp.einsum(eq, part, table, preferred_element_type=jnp.float32)
        else:
            term = jnp.einsum(eq, table, part, preferred_element_type=jnp.float32)
        total = term if total is None else total + term
    return total


def row_windows(kernel, count, block, width):
    padded = jnp.pad(kernel, ((0, width - kernel.shape[0]), (2, width - block - 2)))
    return jnp.concatenate([padded[:, block * w : block * w + width] for w in range(count)], axis=1)


def body(observed, noise_var, row_kernel, col_kernel):
    highest = lax.Precision.HIGH
    rows_axis = ("yh", "z")
    cols_axis = ("x", "yl", "core")
    tile_rows = row_kernel.shape[0]
    tile_cols = col_kernel.shape[0]
    ext_rows = tile_rows + 8
    row_count = axis_count(rows_axis)
    swap = [(0, 1), (1, 0)]
    side = lax.axis_index("yl")
    span = 4 * tile_cols
    quarters = range(col_kernel.shape[1] // span)
    low = jnp.concatenate([col_kernel[:, q * span : q * span + span // 2] for q in quarters], axis=1)
    high = jnp.concatenate([col_kernel[:, q * span + span // 2 : (q + 1) * span] for q in quarters], axis=1)
    near_cols = jnp.where(side == 0, low, high)
    far_cols = jnp.where(side == 0, high, low)
    partner_cols = lax.ppermute(far_cols, "yl", swap)
    row_rows = with_halo(row_kernel, ((rows_axis, 0),), 2)
    row_big = row_windows(row_rows, row_count, tile_rows, ext_rows)
    extended = with_halo(observed, ((cols_axis, 2),), 4)
    col_adj = tap_table(2 * tile_cols + 8, tile_cols, False, 4)
    row_adj = tap_table(ext_rows, 2 * tile_rows, True, 2)
    colsum = exact_dot("rpq,qj->rpj", extended, col_adj, True)
    inducing = exact_dot("ip,rpj->rij", colsum, row_adj, False)
    half = lax.all_gather(inducing, ("x", "core"), axis=2, tiled=True)
    near = jnp.einsum("rik,jk->rij", half, near_cols, precision=highest)
    for_partner = jnp.einsum("rik,jk->rij", half, partner_cols, precision=highest)
    mixed = near + lax.ppermute(for_partner, "yl", swap)
    product = jnp.einsum(
        "ik,rkj->rij", row_big, lax.all_gather(mixed, rows_axis, axis=1, tiled=True), precision=highest
    )
    coarse_ext = with_halo(product, ((cols_axis, 2),), 2)
    row_fwd = tap_table(2 * tile_rows, ext_rows, False, 2)
    col_fwd = tap_table(tile_cols + 4, 2 * tile_cols, True, 2)
    rowpass = exact_dot("pi,rij->rpj", coarse_ext, row_fwd, False)
    result = exact_dot("rpj,jq->rpq", rowpass, col_fwd, True)
    return result + noise_var[None] * observed


def solution(mesh):
    rows_n, cols_n = mesh.devices.shape
    z = min(4, rows_n)
    shape = (rows_n // z, z, cols_n // 4, 2, 2)
    fine = Mesh(mesh.devices.reshape(shape), ("yh", "z", "x", "yl", "core"))
    rows = ("yh", "z")
    cols = ("x", "yl", "core")
    return jax.shard_map(
        body,
        mesh=fine,
        in_specs=(P(None, rows, cols), P(rows, cols), P(rows, None), P(cols, None)),
        out_specs=P(None, rows, cols),
        check_vma=False,
    )
```

```python
import jax
import jax.numpy as jnp
from jax import lax
from jax.sharding import Mesh, PartitionSpec as P


def axis_count(axis):
    return lax.psum(1, axis)


def with_halo(cells, sides, width):
    for axis, dim in sides:
        count = axis_count(axis)
        ends = count - 1
        head = lax.slice_in_dim(cells, 0, width, axis=dim)
        tail = lax.slice_in_dim(cells, cells.shape[dim] - width, cells.shape[dim], axis=dim)
        cells = jnp.concatenate(
            [
                lax.ppermute(tail, axis, [(i, (i + 1) % count) for i in range(ends)]),
                cells,
                lax.ppermute(head, axis, [((i + 1) % count, i) for i in range(ends)]),
            ],
            axis=dim,
        )
    return cells


def keys_weight(dist):
    span = jnp.abs(dist)
    inner = (1.5 * span - 2.5) * span * span + 1.0
    outer = ((-0.5 * span + 2.5) * span - 4.0) * span + 2.0
    return jnp.where(span < 1.0, inner, jnp.where(span < 2.0, outer, 0.0))


def tap_table(rows, cols, coarse_on_rows, pad):
    r = lax.broadcasted_iota(jnp.float32, (rows, cols), 0)
    c = lax.broadcasted_iota(jnp.float32, (rows, cols), 1)
    if coarse_on_rows:
        coarse, fine = r, c
    else:
        coarse, fine = c, r
    if pad == 4:
        dist = coarse - ((fine - 4.0) * 0.5 + 0.25)
    else:
        dist = coarse - 2.0 - (fine * 0.5 + 0.25)
    return keys_weight(dist).astype(jnp.bfloat16)


def split3(x):
    hi = lax.reduce_precision(x, exponent_bits=8, mantissa_bits=7)
    rest = x - hi
    mid = lax.reduce_precision(rest, exponent_bits=8, mantissa_bits=7)
    lo = rest - mid
    return hi.astype(jnp.bfloat16), mid.astype(jnp.bfloat16), lo.astype(jnp.bfloat16)


def exact_dot(eq, x, table, data_first):
    total = None
    for part in split3(x):
        if data_first:
            term = jnp.einsum(eq, part, table, preferred_element_type=jnp.float32)
        else:
            term = jnp.einsum(eq, table, part, preferred_element_type=jnp.float32)
        total = term if total is None else total + term
    return total


def row_windows(kernel, count, block, width):
    padded = jnp.pad(kernel, ((0, width - kernel.shape[0]), (2, width - block - 2)))
    return jnp.concatenate([padded[:, block * w : block * w + width] for w in range(count)], axis=1)


def body(observed, noise_var, row_kernel, col_kernel):
    highest = lax.Precision.HIGH
    rows_axis = ("yh", "z")
    cols_axis = ("x", "yl", "core")
    tile_rows = row_kernel.shape[0]
    tile_cols = col_kernel.shape[0]
    ext_rows = tile_rows + 8
    row_count = axis_count(rows_axis)
    swap = [(0, 1), (1, 0)]
    side = lax.axis_index("yl")
    core = lax.axis_index("core")
    span = 4 * tile_cols
    steps = range(col_kernel.shape[1] // span)

    def quarter(s_idx, c_idx):
        off = (2 * s_idx + c_idx) * tile_cols
        return jnp.concatenate([col_kernel[:, q * span + off : q * span + off + tile_cols] for q in steps], axis=1)

    quarters = [[quarter(0, 0), quarter(0, 1)], [quarter(1, 0), quarter(1, 1)]]

    def pick(s_val, c_val):
        first = jnp.where(c_val == 0, quarters[0][0], quarters[0][1])
        second = jnp.where(c_val == 0, quarters[1][0], quarters[1][1])
        return jnp.where(s_val == 0, first, second)

    diagonal = [(0, 3), (1, 2), (2, 1), (3, 0)]
    own_cols = pick(side, core)
    from_core = lax.ppermute(pick(side, 1 - core), "core", swap)
    from_side = lax.ppermute(pick(1 - side, core), "yl", swap)
    from_diag = lax.ppermute(pick(1 - side, 1 - core), ("yl", "core"), diagonal)
    row_rows = with_halo(row_kernel, ((rows_axis, 0),), 2)
    row_big = row_windows(row_rows, row_count, tile_rows, ext_rows)
    extended = with_halo(observed, ((cols_axis, 2),), 4)
    col_adj = tap_table(2 * tile_cols + 8, tile_cols, False, 4)
    row_adj = tap_table(ext_rows, 2 * tile_rows, True, 2)
    colsum = exact_dot("rpq,qj->rpj", extended, col_adj, True)
    inducing = exact_dot("ip,rpj->rij", colsum, row_adj, False)
    part = lax.all_gather(inducing, "x", axis=2, tiled=True)
    to_side = jnp.einsum("rik,jk->rij", part, from_side, precision=highest)
    to_diag = jnp.einsum("rik,jk->rij", part, from_diag, precision=highest)
    other_chip = to_side + lax.ppermute(to_diag, "core", swap)
    from_other_chip = lax.ppermute(other_chip, "yl", swap)
    own = jnp.einsum("rik,jk->rij", part, own_cols, precision=highest)
    to_core = jnp.einsum("rik,jk->rij", part, from_core, precision=highest)
    mixed = own + lax.ppermute(to_core, "core", swap) + from_other_chip
    product = jnp.einsum(
        "ik,rkj->rij", row_big, lax.all_gather(mixed, rows_axis, axis=1, tiled=True), precision=highest
    )
    coarse_ext = with_halo(product, ((cols_axis, 2),), 2)
    row_fwd = tap_table(2 * tile_rows, ext_rows, False, 2)
    col_fwd = tap_table(tile_cols + 4, 2 * tile_cols, True, 2)
    rowpass = exact_dot("pi,rij->rpj", coarse_ext, row_fwd, False)
    result = exact_dot("rpj,jq->rpq", rowpass, col_fwd, True)
    return result + noise_var[None] * observed


def solution(mesh):
    rows_n, cols_n = mesh.devices.shape
    z = min(4, rows_n)
    shape = (rows_n // z, z, cols_n // 4, 2, 2)
    fine = Mesh(mesh.devices.reshape(shape), ("yh", "z", "x", "yl", "core"))
    rows = ("yh", "z")
    cols = ("x", "yl", "core")
    return jax.shard_map(
        body,
        mesh=fine,
        in_specs=(P(None, rows, cols), P(rows, cols), P(rows, None), P(cols, None)),
        out_specs=P(None, rows, cols),
        check_vma=False,
    )
```

```python
import jax
import jax.numpy as jnp
from jax import lax
from jax.sharding import Mesh, PartitionSpec as P


def axis_count(axis):
    return lax.psum(1, axis)


def with_halo(cells, sides, width):
    for axis, dim in sides:
        count = axis_count(axis)
        ends = count - 1
        head = lax.slice_in_dim(cells, 0, width, axis=dim)
        tail = lax.slice_in_dim(cells, cells.shape[dim] - width, cells.shape[dim], axis=dim)
        cells = jnp.concatenate(
            [
                lax.ppermute(tail, axis, [(i, (i + 1) % count) for i in range(ends)]),
                cells,
                lax.ppermute(head, axis, [((i + 1) % count, i) for i in range(ends)]),
            ],
            axis=dim,
        )
    return cells


def edges(cells, axis, dim, width):
    count = axis_count(axis)
    ends = count - 1
    head = lax.slice_in_dim(cells, 0, width, axis=dim)
    tail = lax.slice_in_dim(cells, cells.shape[dim] - width, cells.shape[dim], axis=dim)
    before = lax.ppermute(tail, axis, [(i, i + 1) for i in range(ends)])
    after = lax.ppermute(head, axis, [(i + 1, i) for i in range(ends)])
    return before, after


def keys_weight(dist):
    span = jnp.abs(dist)
    inner = (1.5 * span - 2.5) * span * span + 1.0
    outer = ((-0.5 * span + 2.5) * span - 4.0) * span + 2.0
    return jnp.where(span < 1.0, inner, jnp.where(span < 2.0, outer, 0.0))


def tap_table(rows, cols, coarse_on_rows, pad):
    r = lax.broadcasted_iota(jnp.float32, (rows, cols), 0)
    c = lax.broadcasted_iota(jnp.float32, (rows, cols), 1)
    if coarse_on_rows:
        coarse, fine = r, c
    else:
        coarse, fine = c, r
    if pad == 4:
        dist = coarse - ((fine - 4.0) * 0.5 + 0.25)
    else:
        dist = coarse - 2.0 - (fine * 0.5 + 0.25)
    return keys_weight(dist).astype(jnp.bfloat16)


def split3(x):
    hi = lax.reduce_precision(x, exponent_bits=8, mantissa_bits=7)
    rest = x - hi
    mid = lax.reduce_precision(rest, exponent_bits=8, mantissa_bits=7)
    lo = rest - mid
    return hi.astype(jnp.bfloat16), mid.astype(jnp.bfloat16), lo.astype(jnp.bfloat16)


def exact_dot(eq, x, table, data_first):
    total = None
    for part in split3(x):
        if data_first:
            term = jnp.einsum(eq, part, table, preferred_element_type=jnp.float32)
        else:
            term = jnp.einsum(eq, table, part, preferred_element_type=jnp.float32)
        total = term if total is None else total + term
    return total


def row_windows(kernel, count, block, width):
    padded = jnp.pad(kernel, ((0, width - kernel.shape[0]), (2, width - block - 2)))
    return jnp.concatenate([padded[:, block * w : block * w + width] for w in range(count)], axis=1)


def body(observed, noise_var, row_kernel, col_kernel):
    highest = lax.Precision.HIGH
    rows_axis = ("yh", "z")
    cols_axis = ("x", "yl", "core")
    tile_rows = row_kernel.shape[0]
    tile_cols = col_kernel.shape[0]
    ext_rows = tile_rows + 8
    row_count = axis_count(rows_axis)
    swap = [(0, 1), (1, 0)]
    side = lax.axis_index("yl")
    span = 4 * tile_cols
    quarters = range(col_kernel.shape[1] // span)
    low = jnp.concatenate([col_kernel[:, q * span : q * span + span // 2] for q in quarters], axis=1)
    high = jnp.concatenate([col_kernel[:, q * span + span // 2 : (q + 1) * span] for q in quarters], axis=1)
    near_cols = jnp.where(side == 0, low, high)
    far_cols = jnp.where(side == 0, high, low)
    partner_cols = lax.ppermute(far_cols, "yl", swap)
    row_rows = with_halo(row_kernel, ((rows_axis, 0),), 2)
    row_big = row_windows(row_rows, row_count, tile_rows, ext_rows)
    before, after = edges(observed, cols_axis, 2, 4)
    col_adj = tap_table(2 * tile_cols + 8, tile_cols, False, 4)
    row_adj = tap_table(ext_rows, 2 * tile_rows, True, 2)
    colsum = (
        exact_dot("rpq,qj->rpj", observed, col_adj[4:-4], True)
        + exact_dot("rpq,qj->rpj", before, col_adj[:4], True)
        + exact_dot("rpq,qj->rpj", after, col_adj[-4:], True)
    )
    inducing = exact_dot("ip,rpj->rij", colsum, row_adj, False)
    half = lax.all_gather(inducing, ("x", "core"), axis=2, tiled=True)
    near = jnp.einsum("rik,jk->rij", half, near_cols, precision=highest)
    for_partner = jnp.einsum("rik,jk->rij", half, partner_cols, precision=highest)
    mixed = near + lax.ppermute(for_partner, "yl", swap)
    product = jnp.einsum(
        "ik,rkj->rij", row_big, lax.all_gather(mixed, rows_axis, axis=1, tiled=True), precision=highest
    )
    before, after = edges(product, cols_axis, 2, 2)
    row_fwd = tap_table(2 * tile_rows, ext_rows, False, 2)
    col_fwd = tap_table(tile_cols + 4, 2 * tile_cols, True, 2)
    result = (
        exact_dot("rpj,jq->rpq", exact_dot("pi,rij->rpj", product, row_fwd, False), col_fwd[2:-2], True)
        + exact_dot("rpj,jq->rpq", exact_dot("pi,rij->rpj", before, row_fwd, False), col_fwd[:2], True)
        + exact_dot("rpj,jq->rpq", exact_dot("pi,rij->rpj", after, row_fwd, False), col_fwd[-2:], True)
    )
    return result + noise_var[None] * observed


def solution(mesh):
    rows_n, cols_n = mesh.devices.shape
    z = min(4, rows_n)
    shape = (rows_n // z, z, cols_n // 4, 2, 2)
    fine = Mesh(mesh.devices.reshape(shape), ("yh", "z", "x", "yl", "core"))
    rows = ("yh", "z")
    cols = ("x", "yl", "core")
    return jax.shard_map(
        body,
        mesh=fine,
        in_specs=(P(None, rows, cols), P(rows, cols), P(rows, None), P(cols, None)),
        out_specs=P(None, rows, cols),
        check_vma=False,
    )
```

```python
import jax
import jax.numpy as jnp
from jax import lax
from jax.sharding import Mesh, PartitionSpec as P


def axis_count(axis):
    return lax.psum(1, axis)


def with_halo(cells, sides, width):
    for axis, dim in sides:
        count = axis_count(axis)
        ends = count - 1
        head = lax.slice_in_dim(cells, 0, width, axis=dim)
        tail = lax.slice_in_dim(cells, cells.shape[dim] - width, cells.shape[dim], axis=dim)
        cells = jnp.concatenate(
            [
                lax.ppermute(tail, axis, [(i, (i + 1) % count) for i in range(ends)]),
                cells,
                lax.ppermute(head, axis, [((i + 1) % count, i) for i in range(ends)]),
            ],
            axis=dim,
        )
    return cells


def edges(cells, axis, dim, width):
    count = axis_count(axis)
    ends = count - 1
    head = lax.slice_in_dim(cells, 0, width, axis=dim)
    tail = lax.slice_in_dim(cells, cells.shape[dim] - width, cells.shape[dim], axis=dim)
    before = lax.ppermute(tail, axis, [(i, i + 1) for i in range(ends)])
    after = lax.ppermute(head, axis, [(i + 1, i) for i in range(ends)])
    return before, after


def keys_weight(dist):
    span = jnp.abs(dist)
    inner = (1.5 * span - 2.5) * span * span + 1.0
    outer = ((-0.5 * span + 2.5) * span - 4.0) * span + 2.0
    return jnp.where(span < 1.0, inner, jnp.where(span < 2.0, outer, 0.0))


def tap_table(rows, cols, coarse_on_rows, pad):
    r = lax.broadcasted_iota(jnp.float32, (rows, cols), 0)
    c = lax.broadcasted_iota(jnp.float32, (rows, cols), 1)
    if coarse_on_rows:
        coarse, fine = r, c
    else:
        coarse, fine = c, r
    if pad == 4:
        dist = coarse - ((fine - 4.0) * 0.5 + 0.25)
    else:
        dist = coarse - 2.0 - (fine * 0.5 + 0.25)
    return keys_weight(dist).astype(jnp.bfloat16)


def split3(x):
    hi = lax.reduce_precision(x, exponent_bits=8, mantissa_bits=7)
    rest = x - hi
    mid = lax.reduce_precision(rest, exponent_bits=8, mantissa_bits=7)
    lo = rest - mid
    return hi.astype(jnp.bfloat16), mid.astype(jnp.bfloat16), lo.astype(jnp.bfloat16)


def exact_dot(eq, x, table, data_first):
    total = None
    for part in split3(x):
        if data_first:
            term = jnp.einsum(eq, part, table, preferred_element_type=jnp.float32)
        else:
            term = jnp.einsum(eq, table, part, preferred_element_type=jnp.float32)
        total = term if total is None else total + term
    return total


def row_windows(kernel, count, block, width):
    padded = jnp.pad(kernel, ((0, width - kernel.shape[0]), (2, width - block - 2)))
    return jnp.concatenate([padded[:, block * w : block * w + width] for w in range(count)], axis=1)


def body(observed, noise_var, row_kernel, col_kernel):
    highest = lax.Precision.HIGH
    rows_axis = ("yh", "z")
    cols_axis = ("x", "yl", "core")
    tile_rows = row_kernel.shape[0]
    tile_cols = col_kernel.shape[0]
    ext_rows = tile_rows + 8
    row_count = axis_count(rows_axis)
    swap = [(0, 1), (1, 0)]
    side = lax.axis_index("yl")
    span = 4 * tile_cols
    quarters = range(col_kernel.shape[1] // span)
    low = jnp.concatenate([col_kernel[:, q * span : q * span + span // 2] for q in quarters], axis=1)
    high = jnp.concatenate([col_kernel[:, q * span + span // 2 : (q + 1) * span] for q in quarters], axis=1)
    near_cols = jnp.where(side == 0, low, high)
    far_cols = jnp.where(side == 0, high, low)
    partner_cols = lax.ppermute(far_cols, "yl", swap)
    row_rows = with_halo(row_kernel, ((rows_axis, 0),), 2)
    row_big = row_windows(row_rows, row_count, tile_rows, ext_rows)
    before, after = edges(observed, cols_axis, 2, 4)
    col_adj = tap_table(2 * tile_cols + 8, tile_cols, False, 4)
    row_adj = tap_table(ext_rows, 2 * tile_rows, True, 2)
    colsum = (
        exact_dot("rpq,qj->rpj", observed, col_adj[4:-4], True)
        + exact_dot("rpq,qj->rpj", before, col_adj[:4], True)
        + exact_dot("rpq,qj->rpj", after, col_adj[-4:], True)
    )
    inducing = exact_dot("ip,rpj->rij", colsum, row_adj, False)
    half = lax.all_gather(inducing, ("x", "core"), axis=2, tiled=True)
    near = jnp.einsum("rik,jk->rij", half, near_cols, precision=highest)
    for_partner = jnp.einsum("rik,jk->rij", half, partner_cols, precision=highest)
    mixed = near + lax.ppermute(for_partner, "yl", swap)
    product = jnp.einsum(
        "ik,rkj->rij", row_big, lax.all_gather(mixed, rows_axis, axis=1, tiled=True), precision=highest
    )
    coarse_ext = with_halo(product, ((cols_axis, 2),), 2)
    row_fwd = tap_table(2 * tile_rows, ext_rows, False, 2)
    col_fwd = tap_table(tile_cols + 4, 2 * tile_cols, True, 2)
    rowpass = exact_dot("pi,rij->rpj", coarse_ext, row_fwd, False)
    result = exact_dot("rpj,jq->rpq", rowpass, col_fwd, True)
    return result + noise_var[None] * observed


def solution(mesh):
    rows_n, cols_n = mesh.devices.shape
    z = min(4, rows_n)
    shape = (rows_n // z, z, cols_n // 4, 2, 2)
    fine = Mesh(mesh.devices.reshape(shape), ("yh", "z", "x", "yl", "core"))
    rows = ("yh", "z")
    cols = ("x", "yl", "core")
    return jax.shard_map(
        body,
        mesh=fine,
        in_specs=(P(None, rows, cols), P(rows, cols), P(rows, None), P(cols, None)),
        out_specs=P(None, rows, cols),
        check_vma=False,
    )
```

```python
import jax
import jax.numpy as jnp
from jax import lax
from jax.sharding import Mesh, PartitionSpec as P


def axis_count(axis):
    return lax.psum(1, axis)


def with_halo(cells, sides, width):
    for axis, dim in sides:
        count = axis_count(axis)
        ends = count - 1
        head = lax.slice_in_dim(cells, 0, width, axis=dim)
        tail = lax.slice_in_dim(cells, cells.shape[dim] - width, cells.shape[dim], axis=dim)
        cells = jnp.concatenate(
            [
                lax.ppermute(tail, axis, [(i, (i + 1) % count) for i in range(ends)]),
                cells,
                lax.ppermute(head, axis, [((i + 1) % count, i) for i in range(ends)]),
            ],
            axis=dim,
        )
    return cells


def edges(cells, axis, dim, width):
    count = axis_count(axis)
    ends = count - 1
    head = lax.slice_in_dim(cells, 0, width, axis=dim)
    tail = lax.slice_in_dim(cells, cells.shape[dim] - width, cells.shape[dim], axis=dim)
    before = lax.ppermute(tail, axis, [(i, i + 1) for i in range(ends)])
    after = lax.ppermute(head, axis, [(i + 1, i) for i in range(ends)])
    return before, after


def keys_weight(dist):
    span = jnp.abs(dist)
    inner = (1.5 * span - 2.5) * span * span + 1.0
    outer = ((-0.5 * span + 2.5) * span - 4.0) * span + 2.0
    return jnp.where(span < 1.0, inner, jnp.where(span < 2.0, outer, 0.0))


def tap_table(rows, cols, coarse_on_rows, pad):
    r = lax.broadcasted_iota(jnp.float32, (rows, cols), 0)
    c = lax.broadcasted_iota(jnp.float32, (rows, cols), 1)
    if coarse_on_rows:
        coarse, fine = r, c
    else:
        coarse, fine = c, r
    if pad == 4:
        dist = coarse - ((fine - 4.0) * 0.5 + 0.25)
    else:
        dist = coarse - 2.0 - (fine * 0.5 + 0.25)
    return keys_weight(dist).astype(jnp.bfloat16)


def split3(x):
    hi = lax.reduce_precision(x, exponent_bits=8, mantissa_bits=7)
    rest = x - hi
    mid = lax.reduce_precision(rest, exponent_bits=8, mantissa_bits=7)
    lo = rest - mid
    return hi.astype(jnp.bfloat16), mid.astype(jnp.bfloat16), lo.astype(jnp.bfloat16)


def exact_dot(eq, x, table, data_first):
    ins, out = eq.split("->")
    first, second = ins.split(",")
    parts = jnp.stack(split3(x))
    if data_first:
        terms = jnp.einsum(f"s{first},{second}->s{out}", parts, table, preferred_element_type=jnp.float32)
    else:
        terms = jnp.einsum(f"{first},s{second}->s{out}", table, parts, preferred_element_type=jnp.float32)
    return terms[0] + terms[1] + terms[2]


def row_windows(kernel, count, block, width):
    padded = jnp.pad(kernel, ((0, width - kernel.shape[0]), (2, width - block - 2)))
    return jnp.concatenate([padded[:, block * w : block * w + width] for w in range(count)], axis=1)


def body(observed, noise_var, row_kernel, col_kernel):
    highest = lax.Precision.HIGH
    rows_axis = ("yh", "z")
    cols_axis = ("x", "yl", "core")
    tile_rows = row_kernel.shape[0]
    tile_cols = col_kernel.shape[0]
    ext_rows = tile_rows + 8
    row_count = axis_count(rows_axis)
    swap = [(0, 1), (1, 0)]
    side = lax.axis_index("yl")
    span = 4 * tile_cols
    quarters = range(col_kernel.shape[1] // span)
    low = jnp.concatenate([col_kernel[:, q * span : q * span + span // 2] for q in quarters], axis=1)
    high = jnp.concatenate([col_kernel[:, q * span + span // 2 : (q + 1) * span] for q in quarters], axis=1)
    near_cols = jnp.where(side == 0, low, high)
    far_cols = jnp.where(side == 0, high, low)
    partner_cols = lax.ppermute(far_cols, "yl", swap)
    row_rows = with_halo(row_kernel, ((rows_axis, 0),), 2)
    row_big = row_windows(row_rows, row_count, tile_rows, ext_rows)
    before, after = edges(observed, cols_axis, 2, 4)
    col_adj = tap_table(2 * tile_cols + 8, tile_cols, False, 4)
    row_adj = tap_table(ext_rows, 2 * tile_rows, True, 2)
    colsum = (
        exact_dot("rpq,qj->rpj", observed, col_adj[4:-4], True)
        + exact_dot("rpq,qj->rpj", before, col_adj[:4], True)
        + exact_dot("rpq,qj->rpj", after, col_adj[-4:], True)
    )
    inducing = exact_dot("ip,rpj->rij", colsum, row_adj, False)
    half = lax.all_gather(inducing, ("x", "core"), axis=2, tiled=True)
    near = jnp.einsum("rik,jk->rij", half, near_cols, precision=highest)
    for_partner = jnp.einsum("rik,jk->rij", half, partner_cols, precision=highest)
    mixed = near + lax.ppermute(for_partner, "yl", swap)
    product = jnp.einsum(
        "ik,rkj->rij", row_big, lax.all_gather(mixed, rows_axis, axis=1, tiled=True), precision=highest
    )
    coarse_ext = with_halo(product, ((cols_axis, 2),), 2)
    row_fwd = tap_table(2 * tile_rows, ext_rows, False, 2)
    col_fwd = tap_table(tile_cols + 4, 2 * tile_cols, True, 2)
    rowpass = exact_dot("pi,rij->rpj", coarse_ext, row_fwd, False)
    result = exact_dot("rpj,jq->rpq", rowpass, col_fwd, True)
    return result + noise_var[None] * observed


def solution(mesh):
    rows_n, cols_n = mesh.devices.shape
    z = min(4, rows_n)
    shape = (rows_n // z, z, cols_n // 4, 2, 2)
    fine = Mesh(mesh.devices.reshape(shape), ("yh", "z", "x", "yl", "core"))
    rows = ("yh", "z")
    cols = ("x", "yl", "core")
    return jax.shard_map(
        body,
        mesh=fine,
        in_specs=(P(None, rows, cols), P(rows, cols), P(rows, None), P(cols, None)),
        out_specs=P(None, rows, cols),
        check_vma=False,
    )
```

```python
import jax
import jax.numpy as jnp
from jax import lax
from jax.sharding import Mesh, PartitionSpec as P


def axis_count(axis):
    return lax.psum(1, axis)


def with_halo(cells, sides, width):
    for axis, dim in sides:
        count = axis_count(axis)
        ends = count - 1
        head = lax.slice_in_dim(cells, 0, width, axis=dim)
        tail = lax.slice_in_dim(cells, cells.shape[dim] - width, cells.shape[dim], axis=dim)
        cells = jnp.concatenate(
            [
                lax.ppermute(tail, axis, [(i, (i + 1) % count) for i in range(ends)]),
                cells,
                lax.ppermute(head, axis, [((i + 1) % count, i) for i in range(ends)]),
            ],
            axis=dim,
        )
    return cells


def edges(cells, axis, dim, width):
    count = axis_count(axis)
    ends = count - 1
    head = lax.slice_in_dim(cells, 0, width, axis=dim)
    tail = lax.slice_in_dim(cells, cells.shape[dim] - width, cells.shape[dim], axis=dim)
    before = lax.ppermute(tail, axis, [(i, i + 1) for i in range(ends)])
    after = lax.ppermute(head, axis, [(i + 1, i) for i in range(ends)])
    return before, after


def keys_weight(dist):
    span = jnp.abs(dist)
    inner = (1.5 * span - 2.5) * span * span + 1.0
    outer = ((-0.5 * span + 2.5) * span - 4.0) * span + 2.0
    return jnp.where(span < 1.0, inner, jnp.where(span < 2.0, outer, 0.0))


def tap_table(rows, cols, coarse_on_rows, pad):
    r = lax.broadcasted_iota(jnp.float32, (rows, cols), 0)
    c = lax.broadcasted_iota(jnp.float32, (rows, cols), 1)
    if coarse_on_rows:
        coarse, fine = r, c
    else:
        coarse, fine = c, r
    if pad == 4:
        dist = coarse - ((fine - 4.0) * 0.5 + 0.25)
    else:
        dist = coarse - 2.0 - (fine * 0.5 + 0.25)
    return keys_weight(dist).astype(jnp.bfloat16)


def split3(x):
    hi = lax.reduce_precision(x, exponent_bits=8, mantissa_bits=7)
    rest = x - hi
    mid = lax.reduce_precision(rest, exponent_bits=8, mantissa_bits=7)
    lo = rest - mid
    return hi.astype(jnp.bfloat16), mid.astype(jnp.bfloat16), lo.astype(jnp.bfloat16)


def exact_dot(eq, x, table, data_first):
    ins, out = eq.split("->")
    first, second = ins.split(",")
    parts = jnp.stack(split3(x))
    if data_first:
        terms = jnp.einsum(f"s{first},{second}->s{out}", parts, table, preferred_element_type=jnp.float32)
    else:
        terms = jnp.einsum(f"{first},s{second}->s{out}", table, parts, preferred_element_type=jnp.float32)
    return terms[0] + terms[1] + terms[2]


def row_windows(kernel, count, block, width):
    padded = jnp.pad(kernel, ((0, width - kernel.shape[0]), (2, width - block - 2)))
    return jnp.concatenate([padded[:, block * w : block * w + width] for w in range(count)], axis=1)


def body(observed, noise_var, row_kernel, col_kernel):
    highest = lax.Precision.HIGH
    rows_axis = ("yh", "z")
    cols_axis = ("x", "yl", "core")
    tile_rows = row_kernel.shape[0]
    tile_cols = col_kernel.shape[0]
    ext_rows = tile_rows + 8
    row_count = axis_count(rows_axis)
    swap = [(0, 1), (1, 0)]
    side = lax.axis_index("yl")
    span = 4 * tile_cols
    quarters = range(col_kernel.shape[1] // span)
    low = jnp.concatenate([col_kernel[:, q * span : q * span + span // 2] for q in quarters], axis=1)
    high = jnp.concatenate([col_kernel[:, q * span + span // 2 : (q + 1) * span] for q in quarters], axis=1)
    near_cols = jnp.where(side == 0, low, high)
    far_cols = jnp.where(side == 0, high, low)
    partner_cols = lax.ppermute(far_cols, "yl", swap)
    row_rows = with_halo(row_kernel, ((rows_axis, 0),), 2)
    row_big = row_windows(row_rows, row_count, tile_rows, ext_rows)
    before, after = edges(observed, cols_axis, 2, 4)
    col_adj = tap_table(2 * tile_cols + 8, tile_cols, False, 4)
    row_adj = tap_table(ext_rows, 2 * tile_rows, True, 2)
    colsum = (
        exact_dot("rpq,qj->rpj", observed, col_adj[4:-4], True)
        + exact_dot("rpq,qj->rpj", before, col_adj[:4], True)
        + exact_dot("rpq,qj->rpj", after, col_adj[-4:], True)
    )
    inducing = exact_dot("ip,rpj->rij", colsum, row_adj, False)
    half = lax.all_gather(inducing, ("x", "core"), axis=2, tiled=True)
    near = jnp.einsum("rik,jk->rij", half, near_cols, precision=highest)
    for_partner = jnp.einsum("rik,jk->rij", half, partner_cols, precision=highest)
    mixed = near + lax.ppermute(for_partner, "yl", swap)
    column_slab = lax.all_gather(mixed, rows_axis, axis=1, tiled=True)
    edge_in = jnp.concatenate([column_slab[..., :2], column_slab[..., -2:]], axis=2)
    edge = jnp.einsum("ik,rkj->rij", row_big, edge_in, precision=highest)
    count = axis_count(cols_axis)
    before = lax.ppermute(edge[..., 2:], cols_axis, [(i, i + 1) for i in range(count - 1)])
    after = lax.ppermute(edge[..., :2], cols_axis, [(i + 1, i) for i in range(count - 1)])
    product = jnp.einsum("ik,rkj->rij", row_big, column_slab, precision=highest)
    coarse_ext = jnp.concatenate([before, product, after], axis=2)
    row_fwd = tap_table(2 * tile_rows, ext_rows, False, 2)
    col_fwd = tap_table(tile_cols + 4, 2 * tile_cols, True, 2)
    rowpass = exact_dot("pi,rij->rpj", coarse_ext, row_fwd, False)
    result = exact_dot("rpj,jq->rpq", rowpass, col_fwd, True)
    return result + noise_var[None] * observed


def solution(mesh):
    rows_n, cols_n = mesh.devices.shape
    z = min(4, rows_n)
    shape = (rows_n // z, z, cols_n // 4, 2, 2)
    fine = Mesh(mesh.devices.reshape(shape), ("yh", "z", "x", "yl", "core"))
    rows = ("yh", "z")
    cols = ("x", "yl", "core")
    return jax.shard_map(
        body,
        mesh=fine,
        in_specs=(P(None, rows, cols), P(rows, cols), P(rows, None), P(cols, None)),
        out_specs=P(None, rows, cols),
        check_vma=False,
    )
```

```python
import jax
import jax.numpy as jnp
from jax import lax
from jax.sharding import Mesh, PartitionSpec as P


def axis_count(axis):
    return lax.psum(1, axis)


def with_halo(cells, sides, width):
    for axis, dim in sides:
        count = axis_count(axis)
        ends = count - 1
        head = lax.slice_in_dim(cells, 0, width, axis=dim)
        tail = lax.slice_in_dim(cells, cells.shape[dim] - width, cells.shape[dim], axis=dim)
        cells = jnp.concatenate(
            [
                lax.ppermute(tail, axis, [(i, (i + 1) % count) for i in range(ends)]),
                cells,
                lax.ppermute(head, axis, [((i + 1) % count, i) for i in range(ends)]),
            ],
            axis=dim,
        )
    return cells


def edges(cells, axis, dim, width):
    count = axis_count(axis)
    ends = count - 1
    head = lax.slice_in_dim(cells, 0, width, axis=dim)
    tail = lax.slice_in_dim(cells, cells.shape[dim] - width, cells.shape[dim], axis=dim)
    before = lax.ppermute(tail, axis, [(i, i + 1) for i in range(ends)])
    after = lax.ppermute(head, axis, [(i + 1, i) for i in range(ends)])
    return before, after


def keys_weight(dist):
    span = jnp.abs(dist)
    inner = (1.5 * span - 2.5) * span * span + 1.0
    outer = ((-0.5 * span + 2.5) * span - 4.0) * span + 2.0
    return jnp.where(span < 1.0, inner, jnp.where(span < 2.0, outer, 0.0))


def tap_table(rows, cols, coarse_on_rows, pad):
    r = lax.broadcasted_iota(jnp.float32, (rows, cols), 0)
    c = lax.broadcasted_iota(jnp.float32, (rows, cols), 1)
    if coarse_on_rows:
        coarse, fine = r, c
    else:
        coarse, fine = c, r
    if pad == 4:
        dist = coarse - ((fine - 4.0) * 0.5 + 0.25)
    else:
        dist = coarse - 2.0 - (fine * 0.5 + 0.25)
    return keys_weight(dist).astype(jnp.bfloat16)


def split3(x):
    hi = lax.reduce_precision(x, exponent_bits=8, mantissa_bits=7)
    rest = x - hi
    mid = lax.reduce_precision(rest, exponent_bits=8, mantissa_bits=7)
    lo = rest - mid
    return hi.astype(jnp.bfloat16), mid.astype(jnp.bfloat16), lo.astype(jnp.bfloat16)


def exact_dot(eq, x, table, data_first):
    ins, out = eq.split("->")
    first, second = ins.split(",")
    parts = jnp.stack(split3(x))
    if data_first:
        terms = jnp.einsum(f"s{first},{second}->s{out}", parts, table, preferred_element_type=jnp.float32)
    else:
        terms = jnp.einsum(f"{first},s{second}->s{out}", table, parts, preferred_element_type=jnp.float32)
    return terms[0] + terms[1] + terms[2]


def row_windows(kernel, order, block, width):
    padded = jnp.pad(kernel, ((0, width - kernel.shape[0]), (2, width - block - 2)))
    return jnp.concatenate([padded[:, block * w : block * w + width] for w in order], axis=1)


def body(observed, noise_var, row_kernel, col_kernel):
    highest = lax.Precision.HIGH
    rows_axis = ("yh", "z")
    cols_axis = ("x", "yl", "core")
    tile_rows = row_kernel.shape[0]
    tile_cols = col_kernel.shape[0]
    ext_rows = tile_rows + 8
    row_count = axis_count(rows_axis)
    swap = [(0, 1), (1, 0)]
    side = lax.axis_index("yl")
    span = 4 * tile_cols
    quarters = range(col_kernel.shape[1] // span)
    low = jnp.concatenate([col_kernel[:, q * span : q * span + span // 2] for q in quarters], axis=1)
    high = jnp.concatenate([col_kernel[:, q * span + span // 2 : (q + 1) * span] for q in quarters], axis=1)
    near_cols = jnp.where(side == 0, low, high)
    far_cols = jnp.where(side == 0, high, low)
    partner_cols = lax.ppermute(far_cols, "yl", swap)
    row_rows = with_halo(row_kernel, ((rows_axis, 0),), 2)
    halves_n = axis_count("yh")
    depth = axis_count("z")
    order = [h * depth + d for d in range(depth) for h in range(halves_n)]
    row_big = row_windows(row_rows, order, tile_rows, ext_rows)
    before, after = edges(observed, cols_axis, 2, 4)
    col_adj = tap_table(2 * tile_cols + 8, tile_cols, False, 4)
    row_adj = tap_table(ext_rows, 2 * tile_rows, True, 2)
    colsum = (
        exact_dot("rpq,qj->rpj", observed, col_adj[4:-4], True)
        + exact_dot("rpq,qj->rpj", before, col_adj[:4], True)
        + exact_dot("rpq,qj->rpj", after, col_adj[-4:], True)
    )
    inducing = exact_dot("ip,rpj->rij", colsum, row_adj, False)
    half = lax.all_gather(inducing, ("x", "core"), axis=2, tiled=True)
    near = jnp.einsum("rik,jk->rij", half, near_cols, precision=highest)
    for_partner = jnp.einsum("rik,jk->rij", half, partner_cols, precision=highest)
    mixed = near + lax.ppermute(for_partner, "yl", swap)
    product = jnp.einsum(
        "ik,rkj->rij", row_big, lax.all_gather(mixed, ("z", "yh"), axis=1, tiled=True), precision=highest
    )
    coarse_ext = with_halo(product, ((cols_axis, 2),), 2)
    row_fwd = tap_table(2 * tile_rows, ext_rows, False, 2)
    col_fwd = tap_table(tile_cols + 4, 2 * tile_cols, True, 2)
    rowpass = exact_dot("pi,rij->rpj", coarse_ext, row_fwd, False)
    result = exact_dot("rpj,jq->rpq", rowpass, col_fwd, True)
    return result + noise_var[None] * observed


def solution(mesh):
    rows_n, cols_n = mesh.devices.shape
    z = min(4, rows_n)
    shape = (rows_n // z, z, cols_n // 4, 2, 2)
    fine = Mesh(mesh.devices.reshape(shape), ("yh", "z", "x", "yl", "core"))
    rows = ("yh", "z")
    cols = ("x", "yl", "core")
    return jax.shard_map(
        body,
        mesh=fine,
        in_specs=(P(None, rows, cols), P(rows, cols), P(rows, None), P(cols, None)),
        out_specs=P(None, rows, cols),
        check_vma=False,
    )
```

```python
import jax
import jax.numpy as jnp
from jax import lax
from jax.sharding import Mesh, PartitionSpec as P


def axis_count(axis):
    return lax.psum(1, axis)


def with_halo(cells, sides, width):
    for axis, dim in sides:
        count = axis_count(axis)
        ends = count - 1
        head = lax.slice_in_dim(cells, 0, width, axis=dim)
        tail = lax.slice_in_dim(cells, cells.shape[dim] - width, cells.shape[dim], axis=dim)
        cells = jnp.concatenate(
            [
                lax.ppermute(tail, axis, [(i, (i + 1) % count) for i in range(ends)]),
                cells,
                lax.ppermute(head, axis, [((i + 1) % count, i) for i in range(ends)]),
            ],
            axis=dim,
        )
    return cells


def edges(cells, axis, dim, width):
    count = axis_count(axis)
    ends = count - 1
    head = lax.slice_in_dim(cells, 0, width, axis=dim)
    tail = lax.slice_in_dim(cells, cells.shape[dim] - width, cells.shape[dim], axis=dim)
    before = lax.ppermute(tail, axis, [(i, i + 1) for i in range(ends)])
    after = lax.ppermute(head, axis, [(i + 1, i) for i in range(ends)])
    return before, after


def keys_weight(dist):
    span = jnp.abs(dist)
    inner = (1.5 * span - 2.5) * span * span + 1.0
    outer = ((-0.5 * span + 2.5) * span - 4.0) * span + 2.0
    return jnp.where(span < 1.0, inner, jnp.where(span < 2.0, outer, 0.0))


def tap_table(rows, cols, coarse_on_rows, pad):
    r = lax.broadcasted_iota(jnp.float32, (rows, cols), 0)
    c = lax.broadcasted_iota(jnp.float32, (rows, cols), 1)
    if coarse_on_rows:
        coarse, fine = r, c
    else:
        coarse, fine = c, r
    if pad == 4:
        dist = coarse - ((fine - 4.0) * 0.5 + 0.25)
    else:
        dist = coarse - 2.0 - (fine * 0.5 + 0.25)
    return keys_weight(dist).astype(jnp.bfloat16)


def split3(x):
    hi = lax.reduce_precision(x, exponent_bits=8, mantissa_bits=7)
    rest = x - hi
    mid = lax.reduce_precision(rest, exponent_bits=8, mantissa_bits=7)
    lo = rest - mid
    return hi.astype(jnp.bfloat16), mid.astype(jnp.bfloat16), lo.astype(jnp.bfloat16)


def exact_dot(eq, x, table, data_first):
    ins, _ = eq.split("->")
    first, second = ins.split(",")
    if data_first:
        parts = jnp.concatenate(split3(x), axis=first.index(second[0]))
        return jnp.einsum(eq, parts, jnp.concatenate([table] * 3, axis=0), preferred_element_type=jnp.float32)
    parts = jnp.concatenate(split3(x), axis=second.index(first[1]))
    return jnp.einsum(eq, jnp.concatenate([table] * 3, axis=1), parts, preferred_element_type=jnp.float32)


def row_windows(kernel, order, block, width):
    padded = jnp.pad(kernel, ((0, width - kernel.shape[0]), (2, width - block - 2)))
    return jnp.concatenate([padded[:, block * w : block * w + width] for w in order], axis=1)


def body(observed, noise_var, row_kernel, col_kernel):
    highest = lax.Precision.HIGH
    rows_axis = ("yh", "z")
    cols_axis = ("x", "yl", "core")
    tile_rows = row_kernel.shape[0]
    tile_cols = col_kernel.shape[0]
    ext_rows = tile_rows + 8
    row_count = axis_count(rows_axis)
    swap = [(0, 1), (1, 0)]
    side = lax.axis_index("yl")
    span = 4 * tile_cols
    quarters = range(col_kernel.shape[1] // span)
    low = jnp.concatenate([col_kernel[:, q * span : q * span + span // 2] for q in quarters], axis=1)
    high = jnp.concatenate([col_kernel[:, q * span + span // 2 : (q + 1) * span] for q in quarters], axis=1)
    near_cols = jnp.where(side == 0, low, high)
    far_cols = jnp.where(side == 0, high, low)
    partner_cols = lax.ppermute(far_cols, "yl", swap)
    row_rows = with_halo(row_kernel, ((rows_axis, 0),), 2)
    halves_n = axis_count("yh")
    depth = axis_count("z")
    order = [h * depth + d for d in range(depth) for h in range(halves_n)]
    row_big = row_windows(row_rows, order, tile_rows, ext_rows)
    before, after = edges(observed, cols_axis, 2, 4)
    col_adj = tap_table(2 * tile_cols + 8, tile_cols, False, 4)
    row_adj = tap_table(ext_rows, 2 * tile_rows, True, 2)
    colsum = (
        exact_dot("rpq,qj->rpj", observed, col_adj[4:-4], True)
        + exact_dot("rpq,qj->rpj", before, col_adj[:4], True)
        + exact_dot("rpq,qj->rpj", after, col_adj[-4:], True)
    )
    inducing = exact_dot("ip,rpj->rij", colsum, row_adj, False)
    half = lax.all_gather(inducing, ("x", "core"), axis=2, tiled=True)
    near = jnp.einsum("rik,jk->rij", half, near_cols, precision=highest)
    for_partner = jnp.einsum("rik,jk->rij", half, partner_cols, precision=highest)
    mixed = near + lax.ppermute(for_partner, "yl", swap)
    product = jnp.einsum(
        "ik,rkj->rij", row_big, lax.all_gather(mixed, ("z", "yh"), axis=1, tiled=True), precision=highest
    )
    coarse_ext = with_halo(product, ((cols_axis, 2),), 2)
    row_fwd = tap_table(2 * tile_rows, ext_rows, False, 2)
    col_fwd = tap_table(tile_cols + 4, 2 * tile_cols, True, 2)
    rowpass = exact_dot("pi,rij->rpj", coarse_ext, row_fwd, False)
    result = exact_dot("rpj,jq->rpq", rowpass, col_fwd, True)
    return result + noise_var[None] * observed


def solution(mesh):
    rows_n, cols_n = mesh.devices.shape
    z = min(4, rows_n)
    shape = (rows_n // z, z, cols_n // 4, 2, 2)
    fine = Mesh(mesh.devices.reshape(shape), ("yh", "z", "x", "yl", "core"))
    rows = ("yh", "z")
    cols = ("x", "yl", "core")
    return jax.shard_map(
        body,
        mesh=fine,
        in_specs=(P(None, rows, cols), P(rows, cols), P(rows, None), P(cols, None)),
        out_specs=P(None, rows, cols),
        check_vma=False,
    )
```

```python
import jax
import jax.numpy as jnp
from jax import lax
from jax.sharding import Mesh, PartitionSpec as P


def axis_count(axis):
    return lax.psum(1, axis)


def with_halo(cells, sides, width):
    for axis, dim in sides:
        count = axis_count(axis)
        ends = count - 1
        head = lax.slice_in_dim(cells, 0, width, axis=dim)
        tail = lax.slice_in_dim(cells, cells.shape[dim] - width, cells.shape[dim], axis=dim)
        cells = jnp.concatenate(
            [
                lax.ppermute(tail, axis, [(i, (i + 1) % count) for i in range(ends)]),
                cells,
                lax.ppermute(head, axis, [((i + 1) % count, i) for i in range(ends)]),
            ],
            axis=dim,
        )
    return cells


def edges(cells, axis, dim, width):
    count = axis_count(axis)
    ends = count - 1
    head = lax.slice_in_dim(cells, 0, width, axis=dim)
    tail = lax.slice_in_dim(cells, cells.shape[dim] - width, cells.shape[dim], axis=dim)
    before = lax.ppermute(tail, axis, [(i, i + 1) for i in range(ends)])
    after = lax.ppermute(head, axis, [(i + 1, i) for i in range(ends)])
    return before, after


def keys_weight(dist):
    span = jnp.abs(dist)
    inner = (1.5 * span - 2.5) * span * span + 1.0
    outer = ((-0.5 * span + 2.5) * span - 4.0) * span + 2.0
    return jnp.where(span < 1.0, inner, jnp.where(span < 2.0, outer, 0.0))


def tap_table(rows, cols, coarse_on_rows, pad):
    r = lax.broadcasted_iota(jnp.float32, (rows, cols), 0)
    c = lax.broadcasted_iota(jnp.float32, (rows, cols), 1)
    if coarse_on_rows:
        coarse, fine = r, c
    else:
        coarse, fine = c, r
    if pad == 4:
        dist = coarse - ((fine - 4.0) * 0.5 + 0.25)
    else:
        dist = coarse - 2.0 - (fine * 0.5 + 0.25)
    return keys_weight(dist).astype(jnp.bfloat16)


def split3(x):
    hi = lax.reduce_precision(x, exponent_bits=8, mantissa_bits=7)
    rest = x - hi
    mid = lax.reduce_precision(rest, exponent_bits=8, mantissa_bits=7)
    lo = rest - mid
    return hi.astype(jnp.bfloat16), mid.astype(jnp.bfloat16), lo.astype(jnp.bfloat16)


def exact_dot(eq, x, table, data_first):
    ins, _ = eq.split("->")
    first, second = ins.split(",")
    if data_first:
        parts = jnp.concatenate(split3(x), axis=first.index(second[0]))
        return jnp.einsum(eq, parts, jnp.concatenate([table] * 3, axis=0), preferred_element_type=jnp.float32)
    parts = jnp.concatenate(split3(x), axis=second.index(first[1]))
    return jnp.einsum(eq, jnp.concatenate([table] * 3, axis=1), parts, preferred_element_type=jnp.float32)


def row_windows(kernel, order, block, width):
    padded = jnp.pad(kernel, ((0, width - kernel.shape[0]), (2, width - block - 2)))
    return jnp.concatenate([padded[:, block * w : block * w + width] for w in order], axis=1)


def body(observed, noise_var, row_kernel, col_kernel):
    highest = lax.Precision.HIGH
    rows_axis = ("yh", "z")
    cols_axis = ("x", "yl", "core")
    tile_rows = row_kernel.shape[0]
    tile_cols = col_kernel.shape[0]
    ext_rows = tile_rows + 8
    row_count = axis_count(rows_axis)
    swap = [(0, 1), (1, 0)]
    side = lax.axis_index("yl")
    span = 4 * tile_cols
    quarters = range(col_kernel.shape[1] // span)
    low = jnp.concatenate([col_kernel[:, q * span : q * span + span // 2] for q in quarters], axis=1)
    high = jnp.concatenate([col_kernel[:, q * span + span // 2 : (q + 1) * span] for q in quarters], axis=1)
    near_cols = jnp.where(side == 0, low, high)
    far_cols = jnp.where(side == 0, high, low)
    partner_cols = lax.ppermute(far_cols, "yl", swap)
    row_rows = with_halo(row_kernel, ((rows_axis, 0),), 2)
    halves_n = axis_count("yh")
    depth = axis_count("z")
    order = [h * depth + d for d in range(depth) for h in range(halves_n)]
    row_big = row_windows(row_rows, order, tile_rows, ext_rows)
    before, after = edges(observed, cols_axis, 2, 4)
    noisy = lax.optimization_barrier(noise_var[None] * observed)
    col_adj = tap_table(2 * tile_cols + 8, tile_cols, False, 4)
    row_adj = tap_table(ext_rows, 2 * tile_rows, True, 2)
    colsum = (
        exact_dot("rpq,qj->rpj", observed, col_adj[4:-4], True)
        + exact_dot("rpq,qj->rpj", before, col_adj[:4], True)
        + exact_dot("rpq,qj->rpj", after, col_adj[-4:], True)
    )
    inducing = exact_dot("ip,rpj->rij", colsum, row_adj, False)
    half = lax.all_gather(inducing, ("x", "core"), axis=2, tiled=True)
    near = jnp.einsum("rik,jk->rij", half, near_cols, precision=highest)
    for_partner = jnp.einsum("rik,jk->rij", half, partner_cols, precision=highest)
    mixed = near + lax.ppermute(for_partner, "yl", swap)
    product = jnp.einsum(
        "ik,rkj->rij", row_big, lax.all_gather(mixed, ("z", "yh"), axis=1, tiled=True), precision=highest
    )
    coarse_ext = with_halo(product, ((cols_axis, 2),), 2)
    row_fwd = tap_table(2 * tile_rows, ext_rows, False, 2)
    col_fwd = tap_table(tile_cols + 4, 2 * tile_cols, True, 2)
    rowpass = exact_dot("pi,rij->rpj", coarse_ext, row_fwd, False)
    result = exact_dot("rpj,jq->rpq", rowpass, col_fwd, True)
    return result + noisy


def solution(mesh):
    rows_n, cols_n = mesh.devices.shape
    z = min(4, rows_n)
    shape = (rows_n // z, z, cols_n // 4, 2, 2)
    fine = Mesh(mesh.devices.reshape(shape), ("yh", "z", "x", "yl", "core"))
    rows = ("yh", "z")
    cols = ("x", "yl", "core")
    return jax.shard_map(
        body,
        mesh=fine,
        in_specs=(P(None, rows, cols), P(rows, cols), P(rows, None), P(cols, None)),
        out_specs=P(None, rows, cols),
        check_vma=False,
    )
```

```python
import jax
import jax.numpy as jnp
from jax import lax
from jax.sharding import Mesh, PartitionSpec as P


def axis_count(axis):
    return lax.psum(1, axis)


def with_halo(cells, sides, width):
    for axis, dim in sides:
        count = axis_count(axis)
        ends = count - 1
        head = lax.slice_in_dim(cells, 0, width, axis=dim)
        tail = lax.slice_in_dim(cells, cells.shape[dim] - width, cells.shape[dim], axis=dim)
        cells = jnp.concatenate(
            [
                lax.ppermute(tail, axis, [(i, (i + 1) % count) for i in range(ends)]),
                cells,
                lax.ppermute(head, axis, [((i + 1) % count, i) for i in range(ends)]),
            ],
            axis=dim,
        )
    return cells


def edges(cells, axis, dim, width):
    count = axis_count(axis)
    ends = count - 1
    head = lax.slice_in_dim(cells, 0, width, axis=dim)
    tail = lax.slice_in_dim(cells, cells.shape[dim] - width, cells.shape[dim], axis=dim)
    before = lax.ppermute(tail, axis, [(i, i + 1) for i in range(ends)])
    after = lax.ppermute(head, axis, [(i + 1, i) for i in range(ends)])
    return before, after


def keys_weight(dist):
    span = jnp.abs(dist)
    inner = (1.5 * span - 2.5) * span * span + 1.0
    outer = ((-0.5 * span + 2.5) * span - 4.0) * span + 2.0
    return jnp.where(span < 1.0, inner, jnp.where(span < 2.0, outer, 0.0))


def tap_table(rows, cols, coarse_on_rows, pad):
    r = lax.broadcasted_iota(jnp.float32, (rows, cols), 0)
    c = lax.broadcasted_iota(jnp.float32, (rows, cols), 1)
    if coarse_on_rows:
        coarse, fine = r, c
    else:
        coarse, fine = c, r
    if pad == 4:
        dist = coarse - ((fine - 4.0) * 0.5 + 0.25)
    else:
        dist = coarse - 2.0 - (fine * 0.5 + 0.25)
    return keys_weight(dist).astype(jnp.bfloat16)


def split3(x):
    hi = lax.reduce_precision(x, exponent_bits=8, mantissa_bits=7)
    rest = x - hi
    mid = lax.reduce_precision(rest, exponent_bits=8, mantissa_bits=7)
    lo = rest - mid
    return hi.astype(jnp.bfloat16), mid.astype(jnp.bfloat16), lo.astype(jnp.bfloat16)


def exact_dot(eq, x, table, data_first):
    ins, _ = eq.split("->")
    first, second = ins.split(",")
    if data_first:
        parts = jnp.concatenate(split3(x), axis=first.index(second[0]))
        return jnp.einsum(eq, parts, jnp.concatenate([table] * 3, axis=0), preferred_element_type=jnp.float32)
    parts = jnp.concatenate(split3(x), axis=second.index(first[1]))
    return jnp.einsum(eq, jnp.concatenate([table] * 3, axis=1), parts, preferred_element_type=jnp.float32)


def row_windows(kernel, order, block, width):
    padded = jnp.pad(kernel, ((0, width - kernel.shape[0]), (2, width - block - 2)))
    return jnp.concatenate([padded[:, block * w : block * w + width] for w in order], axis=1)


def body(observed, noise_var, row_kernel, col_kernel):
    highest = lax.Precision.HIGH
    rows_axis = ("yh", "z")
    cols_axis = ("x", "yl", "core")
    tile_rows = row_kernel.shape[0]
    tile_cols = col_kernel.shape[0]
    ext_rows = tile_rows + 8
    row_count = axis_count(rows_axis)
    swap = [(0, 1), (1, 0)]
    side = lax.axis_index("yl")
    span = 4 * tile_cols
    quarters = range(col_kernel.shape[1] // span)
    low = jnp.concatenate([col_kernel[:, q * span : q * span + span // 2] for q in quarters], axis=1)
    high = jnp.concatenate([col_kernel[:, q * span + span // 2 : (q + 1) * span] for q in quarters], axis=1)
    near_cols = jnp.where(side == 0, low, high)
    far_cols = jnp.where(side == 0, high, low)
    partner_cols = lax.ppermute(far_cols, "yl", swap)
    row_rows = with_halo(row_kernel, ((rows_axis, 0),), 2)
    halves_n = axis_count("yh")
    depth = axis_count("z")
    order = [h * depth + d for d in range(depth) for h in range(halves_n)]
    row_big = row_windows(row_rows, order, tile_rows, ext_rows)
    before, after = edges(observed, cols_axis, 2, 4)
    col_adj = tap_table(2 * tile_cols + 8, tile_cols, False, 4)
    row_adj = tap_table(ext_rows, 2 * tile_rows, True, 2)
    colsum = (
        exact_dot("rpq,qj->rpj", observed, col_adj[4:-4], True)
        + exact_dot("rpq,qj->rpj", before, col_adj[:4], True)
        + exact_dot("rpq,qj->rpj", after, col_adj[-4:], True)
    )
    inducing = exact_dot("ip,rpj->rij", colsum, row_adj, False)
    half = lax.all_gather(inducing, ("x", "core"), axis=2, tiled=True)
    near = jnp.einsum("rik,jk->rij", half, near_cols, precision=highest)
    for_partner = jnp.einsum("rik,jk->rij", half, partner_cols, precision=highest)
    mixed = near + lax.ppermute(for_partner, "yl", swap)
    product = jnp.einsum(
        "ik,rkj->rij", row_big, lax.all_gather(mixed, ("z", "yh"), axis=1, tiled=True), precision=highest
    )
    before, after = edges(product, cols_axis, 2, 2)
    row_fwd = tap_table(2 * tile_rows, ext_rows, False, 2)
    col_fwd = tap_table(tile_cols + 4, 2 * tile_cols, True, 2)
    rowpass = jnp.concatenate(
        [exact_dot("pi,rij->rpj", cells, row_fwd, False) for cells in (before, product, after)], axis=2
    )
    result = exact_dot("rpj,jq->rpq", rowpass, col_fwd, True)
    return result + noise_var[None] * observed


def solution(mesh):
    rows_n, cols_n = mesh.devices.shape
    z = min(4, rows_n)
    shape = (rows_n // z, z, cols_n // 4, 2, 2)
    fine = Mesh(mesh.devices.reshape(shape), ("yh", "z", "x", "yl", "core"))
    rows = ("yh", "z")
    cols = ("x", "yl", "core")
    return jax.shard_map(
        body,
        mesh=fine,
        in_specs=(P(None, rows, cols), P(rows, cols), P(rows, None), P(cols, None)),
        out_specs=P(None, rows, cols),
        check_vma=False,
    )
```

```python
import jax
import jax.numpy as jnp
from jax import lax
from jax.sharding import Mesh, PartitionSpec as P


def axis_count(axis):
    return lax.psum(1, axis)


def with_halo(cells, sides, width):
    for axis, dim in sides:
        count = axis_count(axis)
        ends = count - 1
        head = lax.slice_in_dim(cells, 0, width, axis=dim)
        tail = lax.slice_in_dim(cells, cells.shape[dim] - width, cells.shape[dim], axis=dim)
        cells = jnp.concatenate(
            [
                lax.ppermute(tail, axis, [(i, (i + 1) % count) for i in range(ends)]),
                cells,
                lax.ppermute(head, axis, [((i + 1) % count, i) for i in range(ends)]),
            ],
            axis=dim,
        )
    return cells


def edges(cells, axis, dim, width):
    count = axis_count(axis)
    ends = count - 1
    head = lax.slice_in_dim(cells, 0, width, axis=dim)
    tail = lax.slice_in_dim(cells, cells.shape[dim] - width, cells.shape[dim], axis=dim)
    before = lax.ppermute(tail, axis, [(i, i + 1) for i in range(ends)])
    after = lax.ppermute(head, axis, [(i + 1, i) for i in range(ends)])
    return before, after


def keys_weight(dist):
    span = jnp.abs(dist)
    inner = (1.5 * span - 2.5) * span * span + 1.0
    outer = ((-0.5 * span + 2.5) * span - 4.0) * span + 2.0
    return jnp.where(span < 1.0, inner, jnp.where(span < 2.0, outer, 0.0))


def tap_table(rows, cols, coarse_on_rows, pad):
    r = lax.broadcasted_iota(jnp.float32, (rows, cols), 0)
    c = lax.broadcasted_iota(jnp.float32, (rows, cols), 1)
    if coarse_on_rows:
        coarse, fine = r, c
    else:
        coarse, fine = c, r
    if pad == 4:
        dist = coarse - ((fine - 4.0) * 0.5 + 0.25)
    else:
        dist = coarse - 2.0 - (fine * 0.5 + 0.25)
    return keys_weight(dist).astype(jnp.bfloat16)


def split3(x):
    hi = lax.reduce_precision(x, exponent_bits=8, mantissa_bits=7)
    rest = x - hi
    mid = lax.reduce_precision(rest, exponent_bits=8, mantissa_bits=7)
    lo = rest - mid
    return hi.astype(jnp.bfloat16), mid.astype(jnp.bfloat16), lo.astype(jnp.bfloat16)


def exact_dot(eq, x, table, data_first):
    ins, _ = eq.split("->")
    first, second = ins.split(",")
    if data_first:
        parts = jnp.concatenate(split3(x), axis=first.index(second[0]))
        return jnp.einsum(eq, parts, jnp.concatenate([table] * 3, axis=0), preferred_element_type=jnp.float32)
    parts = jnp.concatenate(split3(x), axis=second.index(first[1]))
    return jnp.einsum(eq, jnp.concatenate([table] * 3, axis=1), parts, preferred_element_type=jnp.float32)


def row_windows(kernel, order, block, width):
    padded = jnp.pad(kernel, ((0, width - kernel.shape[0]), (2, width - block - 2)))
    return jnp.concatenate([padded[:, block * w : block * w + width] for w in order], axis=1)


def body(observed, noise_var, row_kernel, col_kernel):
    highest = lax.Precision.HIGH
    rows_axis = ("yh", "z")
    cols_axis = ("x", "yl", "core")
    tile_rows = row_kernel.shape[0]
    tile_cols = col_kernel.shape[0]
    ext_rows = tile_rows + 8
    row_count = axis_count(rows_axis)
    swap = [(0, 1), (1, 0)]
    side = lax.axis_index("yl")
    span = 4 * tile_cols
    quarters = range(col_kernel.shape[1] // span)
    low = jnp.concatenate([col_kernel[:, q * span : q * span + span // 2] for q in quarters], axis=1)
    high = jnp.concatenate([col_kernel[:, q * span + span // 2 : (q + 1) * span] for q in quarters], axis=1)
    near_cols = jnp.where(side == 0, low, high)
    far_cols = jnp.where(side == 0, high, low)
    partner_cols = lax.ppermute(far_cols, "yl", swap)
    row_rows = with_halo(row_kernel, ((rows_axis, 0),), 2)
    halves_n = axis_count("yh")
    depth = axis_count("z")
    order = [h * depth + d for d in range(depth) for h in range(halves_n)]
    row_big = row_windows(row_rows, order, tile_rows, ext_rows)
    before, after = edges(observed, cols_axis, 2, 4)
    col_adj = tap_table(2 * tile_cols + 8, tile_cols, False, 4)
    row_adj = tap_table(ext_rows, 2 * tile_rows, True, 2)
    colsum = (
        exact_dot("rpq,qj->rpj", observed, col_adj[4:-4], True)
        + exact_dot("rpq,qj->rpj", before, col_adj[:4], True)
        + exact_dot("rpq,qj->rpj", after, col_adj[-4:], True)
    )
    inducing = exact_dot("ip,rpj->rij", colsum, row_adj, False)
    half = lax.all_gather(inducing, ("x", "core"), axis=2, tiled=True)
    from_partner = [
        lax.ppermute(jnp.einsum("ik,jk->ij", one, partner_cols, precision=highest), "yl", swap) for one in half
    ]
    near = jnp.einsum("rik,jk->rij", half, near_cols, precision=highest)
    mixed = near + jnp.stack(from_partner)
    product = jnp.einsum(
        "ik,rkj->rij", row_big, lax.all_gather(mixed, ("z", "yh"), axis=1, tiled=True), precision=highest
    )
    coarse_ext = with_halo(product, ((cols_axis, 2),), 2)
    row_fwd = tap_table(2 * tile_rows, ext_rows, False, 2)
    col_fwd = tap_table(tile_cols + 4, 2 * tile_cols, True, 2)
    rowpass = exact_dot("pi,rij->rpj", coarse_ext, row_fwd, False)
    result = exact_dot("rpj,jq->rpq", rowpass, col_fwd, True)
    return result + noise_var[None] * observed


def solution(mesh):
    rows_n, cols_n = mesh.devices.shape
    z = min(4, rows_n)
    shape = (rows_n // z, z, cols_n // 4, 2, 2)
    fine = Mesh(mesh.devices.reshape(shape), ("yh", "z", "x", "yl", "core"))
    rows = ("yh", "z")
    cols = ("x", "yl", "core")
    return jax.shard_map(
        body,
        mesh=fine,
        in_specs=(P(None, rows, cols), P(rows, cols), P(rows, None), P(cols, None)),
        out_specs=P(None, rows, cols),
        check_vma=False,
    )
```

```python
import jax
import jax.numpy as jnp
from jax import lax
from jax.sharding import Mesh, PartitionSpec as P


def axis_count(axis):
    return lax.psum(1, axis)


def with_halo(cells, sides, width):
    for axis, dim in sides:
        count = axis_count(axis)
        ends = count - 1
        head = lax.slice_in_dim(cells, 0, width, axis=dim)
        tail = lax.slice_in_dim(cells, cells.shape[dim] - width, cells.shape[dim], axis=dim)
        cells = jnp.concatenate(
            [
                lax.ppermute(tail, axis, [(i, (i + 1) % count) for i in range(ends)]),
                cells,
                lax.ppermute(head, axis, [((i + 1) % count, i) for i in range(ends)]),
            ],
            axis=dim,
        )
    return cells


def edges(cells, axis, dim, width):
    count = axis_count(axis)
    ends = count - 1
    head = lax.slice_in_dim(cells, 0, width, axis=dim)
    tail = lax.slice_in_dim(cells, cells.shape[dim] - width, cells.shape[dim], axis=dim)
    before = lax.ppermute(tail, axis, [(i, i + 1) for i in range(ends)])
    after = lax.ppermute(head, axis, [(i + 1, i) for i in range(ends)])
    return before, after


def keys_weight(dist):
    span = jnp.abs(dist)
    inner = (1.5 * span - 2.5) * span * span + 1.0
    outer = ((-0.5 * span + 2.5) * span - 4.0) * span + 2.0
    return jnp.where(span < 1.0, inner, jnp.where(span < 2.0, outer, 0.0))


def tap_table(rows, cols, coarse_on_rows, pad):
    r = lax.broadcasted_iota(jnp.float32, (rows, cols), 0)
    c = lax.broadcasted_iota(jnp.float32, (rows, cols), 1)
    if coarse_on_rows:
        coarse, fine = r, c
    else:
        coarse, fine = c, r
    if pad == 4:
        dist = coarse - ((fine - 4.0) * 0.5 + 0.25)
    else:
        dist = coarse - 2.0 - (fine * 0.5 + 0.25)
    return keys_weight(dist).astype(jnp.bfloat16)


def split3(x):
    hi = lax.reduce_precision(x, exponent_bits=8, mantissa_bits=7)
    rest = x - hi
    mid = lax.reduce_precision(rest, exponent_bits=8, mantissa_bits=7)
    lo = rest - mid
    return hi.astype(jnp.bfloat16), mid.astype(jnp.bfloat16), lo.astype(jnp.bfloat16)


def exact_dot(eq, x, table, data_first):
    ins, _ = eq.split("->")
    first, second = ins.split(",")
    if data_first:
        parts = jnp.concatenate(split3(x), axis=first.index(second[0]))
        return jnp.einsum(eq, parts, jnp.concatenate([table] * 3, axis=0), preferred_element_type=jnp.float32)
    parts = jnp.concatenate(split3(x), axis=second.index(first[1]))
    return jnp.einsum(eq, jnp.concatenate([table] * 3, axis=1), parts, preferred_element_type=jnp.float32)


def row_windows(kernel, order, block, width):
    padded = jnp.pad(kernel, ((0, width - kernel.shape[0]), (2, width - block - 2)))
    return jnp.concatenate([padded[:, block * w : block * w + width] for w in order], axis=1)


def body(observed, noise_var, row_kernel, col_kernel):
    highest = lax.Precision.HIGH
    rows_axis = ("yh", "z")
    cols_axis = ("x", "yl", "core")
    tile_rows = row_kernel.shape[0]
    tile_cols = col_kernel.shape[0]
    ext_rows = tile_rows + 8
    row_count = axis_count(rows_axis)
    swap = [(0, 1), (1, 0)]
    side = lax.axis_index("yl")
    span = 4 * tile_cols
    quarters = range(col_kernel.shape[1] // span)
    low = jnp.concatenate([col_kernel[:, q * span : q * span + span // 2] for q in quarters], axis=1)
    high = jnp.concatenate([col_kernel[:, q * span + span // 2 : (q + 1) * span] for q in quarters], axis=1)
    near_cols = jnp.where(side == 0, low, high)
    far_cols = jnp.where(side == 0, high, low)
    partner_cols = lax.ppermute(far_cols, "yl", swap)
    row_rows = with_halo(row_kernel, ((rows_axis, 0),), 2)
    halves_n = axis_count("yh")
    depth = axis_count("z")
    order = [h * depth + d for d in range(depth) for h in range(halves_n)]
    row_big = row_windows(row_rows, order, tile_rows, ext_rows)
    before, after = edges(observed, cols_axis, 2, 4)
    col_adj = tap_table(2 * tile_cols + 8, tile_cols, False, 4)
    row_adj = tap_table(ext_rows, 2 * tile_rows, True, 2)
    colsum = (
        exact_dot("rpq,qj->rpj", observed, col_adj[4:-4], True)
        + exact_dot("rpq,qj->rpj", before, col_adj[:4], True)
        + exact_dot("rpq,qj->rpj", after, col_adj[-4:], True)
    )
    inducing = exact_dot("ip,rpj->rij", colsum, row_adj, False)
    half = lax.all_gather(inducing, ("x", "core"), axis=2, tiled=True)
    near = jnp.einsum("rik,jk->rij", half, near_cols, precision=highest)
    for_partner = jnp.einsum("rik,jk->rij", half, partner_cols, precision=highest)
    mixed = near + lax.ppermute(for_partner, "yl", swap)
    kernel_hi = lax.reduce_precision(row_big, exponent_bits=8, mantissa_bits=7)
    kernel_parts = jnp.concatenate([kernel_hi, kernel_hi, row_big - kernel_hi], axis=1).astype(jnp.bfloat16)
    column_slab = lax.all_gather(mixed, ("z", "yh"), axis=1, tiled=True)
    slab_hi = lax.reduce_precision(column_slab, exponent_bits=8, mantissa_bits=7)
    slab_parts = jnp.concatenate([slab_hi, column_slab - slab_hi, slab_hi], axis=1).astype(jnp.bfloat16)
    product = jnp.einsum("ik,rkj->rij", kernel_parts, slab_parts, preferred_element_type=jnp.float32)
    coarse_ext = with_halo(product, ((cols_axis, 2),), 2)
    row_fwd = tap_table(2 * tile_rows, ext_rows, False, 2)
    col_fwd = tap_table(tile_cols + 4, 2 * tile_cols, True, 2)
    rowpass = exact_dot("pi,rij->rpj", coarse_ext, row_fwd, False)
    result = exact_dot("rpj,jq->rpq", rowpass, col_fwd, True)
    return result + noise_var[None] * observed


def solution(mesh):
    rows_n, cols_n = mesh.devices.shape
    z = min(4, rows_n)
    shape = (rows_n // z, z, cols_n // 4, 2, 2)
    fine = Mesh(mesh.devices.reshape(shape), ("yh", "z", "x", "yl", "core"))
    rows = ("yh", "z")
    cols = ("x", "yl", "core")
    return jax.shard_map(
        body,
        mesh=fine,
        in_specs=(P(None, rows, cols), P(rows, cols), P(rows, None), P(cols, None)),
        out_specs=P(None, rows, cols),
        check_vma=False,
    )
```

```python
import jax
import jax.numpy as jnp
from jax import lax
from jax.sharding import Mesh, PartitionSpec as P


def axis_count(axis):
    return lax.psum(1, axis)


def with_halo(cells, sides, width):
    for axis, dim in sides:
        count = axis_count(axis)
        ends = count - 1
        head = lax.slice_in_dim(cells, 0, width, axis=dim)
        tail = lax.slice_in_dim(cells, cells.shape[dim] - width, cells.shape[dim], axis=dim)
        cells = jnp.concatenate(
            [
                lax.ppermute(tail, axis, [(i, (i + 1) % count) for i in range(ends)]),
                cells,
                lax.ppermute(head, axis, [((i + 1) % count, i) for i in range(ends)]),
            ],
            axis=dim,
        )
    return cells


def edges(cells, axis, dim, width):
    count = axis_count(axis)
    ends = count - 1
    head = lax.slice_in_dim(cells, 0, width, axis=dim)
    tail = lax.slice_in_dim(cells, cells.shape[dim] - width, cells.shape[dim], axis=dim)
    before = lax.ppermute(tail, axis, [(i, i + 1) for i in range(ends)])
    after = lax.ppermute(head, axis, [(i + 1, i) for i in range(ends)])
    return before, after


def keys_weight(dist):
    span = jnp.abs(dist)
    inner = (1.5 * span - 2.5) * span * span + 1.0
    outer = ((-0.5 * span + 2.5) * span - 4.0) * span + 2.0
    return jnp.where(span < 1.0, inner, jnp.where(span < 2.0, outer, 0.0))


def tap_table(rows, cols, coarse_on_rows, pad):
    r = lax.broadcasted_iota(jnp.float32, (rows, cols), 0)
    c = lax.broadcasted_iota(jnp.float32, (rows, cols), 1)
    if coarse_on_rows:
        coarse, fine = r, c
    else:
        coarse, fine = c, r
    if pad == 4:
        dist = coarse - ((fine - 4.0) * 0.5 + 0.25)
    else:
        dist = coarse - 2.0 - (fine * 0.5 + 0.25)
    return keys_weight(dist).astype(jnp.bfloat16)


def split3(x):
    hi = lax.reduce_precision(x, exponent_bits=8, mantissa_bits=7)
    rest = x - hi
    mid = lax.reduce_precision(rest, exponent_bits=8, mantissa_bits=7)
    lo = rest - mid
    return hi.astype(jnp.bfloat16), mid.astype(jnp.bfloat16), lo.astype(jnp.bfloat16)


def exact_dot(eq, x, table, data_first):
    ins, _ = eq.split("->")
    first, second = ins.split(",")
    if data_first:
        parts = jnp.concatenate(split3(x), axis=first.index(second[0]))
        return jnp.einsum(eq, parts, jnp.concatenate([table] * 3, axis=0), preferred_element_type=jnp.float32)
    parts = jnp.concatenate(split3(x), axis=second.index(first[1]))
    return jnp.einsum(eq, jnp.concatenate([table] * 3, axis=1), parts, preferred_element_type=jnp.float32)


def row_windows(kernel, order, block, width):
    padded = jnp.pad(kernel, ((0, width - kernel.shape[0]), (2, width - block - 2)))
    return jnp.concatenate([padded[:, block * w : block * w + width] for w in order], axis=1)


def body(observed, noise_var, row_kernel, col_kernel):
    highest = lax.Precision.HIGH
    rows_axis = ("yh", "z")
    cols_axis = ("x", "yl", "core")
    tile_rows = row_kernel.shape[0]
    tile_cols = col_kernel.shape[0]
    ext_rows = tile_rows + 8
    row_count = axis_count(rows_axis)
    swap = [(0, 1), (1, 0)]
    side = lax.axis_index("yl")
    span = 4 * tile_cols
    quarters = range(col_kernel.shape[1] // span)
    def half_cols(s_idx):
        starts = [q * span + s_idx * span // 2 + c * tile_cols for c in range(2) for q in quarters]
        return jnp.concatenate([col_kernel[:, a : a + tile_cols] for a in starts], axis=1)

    low = half_cols(0)
    high = half_cols(1)
    near_cols = jnp.where(side == 0, low, high)
    far_cols = jnp.where(side == 0, high, low)
    partner_cols = lax.ppermute(far_cols, "yl", swap)
    row_rows = with_halo(row_kernel, ((rows_axis, 0),), 2)
    halves_n = axis_count("yh")
    depth = axis_count("z")
    order = [h * depth + d for d in range(depth) for h in range(halves_n)]
    row_big = row_windows(row_rows, order, tile_rows, ext_rows)
    before, after = edges(observed, cols_axis, 2, 4)
    col_adj = tap_table(2 * tile_cols + 8, tile_cols, False, 4)
    row_adj = tap_table(ext_rows, 2 * tile_rows, True, 2)
    colsum = (
        exact_dot("rpq,qj->rpj", observed, col_adj[4:-4], True)
        + exact_dot("rpq,qj->rpj", before, col_adj[:4], True)
        + exact_dot("rpq,qj->rpj", after, col_adj[-4:], True)
    )
    inducing = exact_dot("ip,rpj->rij", colsum, row_adj, False)
    half = lax.all_gather(inducing, ("core", "x"), axis=2, tiled=True)
    near = jnp.einsum("rik,jk->rij", half, near_cols, precision=highest)
    for_partner = jnp.einsum("rik,jk->rij", half, partner_cols, precision=highest)
    mixed = near + lax.ppermute(for_partner, "yl", swap)
    product = jnp.einsum(
        "ik,rkj->rij", row_big, lax.all_gather(mixed, ("z", "yh"), axis=1, tiled=True), precision=highest
    )
    coarse_ext = with_halo(product, ((cols_axis, 2),), 2)
    row_fwd = tap_table(2 * tile_rows, ext_rows, False, 2)
    col_fwd = tap_table(tile_cols + 4, 2 * tile_cols, True, 2)
    rowpass = exact_dot("pi,rij->rpj", coarse_ext, row_fwd, False)
    result = exact_dot("rpj,jq->rpq", rowpass, col_fwd, True)
    return result + noise_var[None] * observed


def solution(mesh):
    rows_n, cols_n = mesh.devices.shape
    z = min(4, rows_n)
    shape = (rows_n // z, z, cols_n // 4, 2, 2)
    fine = Mesh(mesh.devices.reshape(shape), ("yh", "z", "x", "yl", "core"))
    rows = ("yh", "z")
    cols = ("x", "yl", "core")
    return jax.shard_map(
        body,
        mesh=fine,
        in_specs=(P(None, rows, cols), P(rows, cols), P(rows, None), P(cols, None)),
        out_specs=P(None, rows, cols),
        check_vma=False,
    )
```

```python
import jax
import jax.numpy as jnp
from jax import lax
from jax.sharding import Mesh, PartitionSpec as P


def axis_count(axis):
    return lax.psum(1, axis)


def with_halo(cells, sides, width):
    for axis, dim in sides:
        count = axis_count(axis)
        ends = count - 1
        head = lax.slice_in_dim(cells, 0, width, axis=dim)
        tail = lax.slice_in_dim(cells, cells.shape[dim] - width, cells.shape[dim], axis=dim)
        cells = jnp.concatenate(
            [
                lax.ppermute(tail, axis, [(i, (i + 1) % count) for i in range(ends)]),
                cells,
                lax.ppermute(head, axis, [((i + 1) % count, i) for i in range(ends)]),
            ],
            axis=dim,
        )
    return cells


def edges(cells, axis, dim, width):
    count = axis_count(axis)
    ends = count - 1
    head = lax.slice_in_dim(cells, 0, width, axis=dim)
    tail = lax.slice_in_dim(cells, cells.shape[dim] - width, cells.shape[dim], axis=dim)
    before = lax.ppermute(tail, axis, [(i, i + 1) for i in range(ends)])
    after = lax.ppermute(head, axis, [(i + 1, i) for i in range(ends)])
    return before, after


def keys_weight(dist):
    span = jnp.abs(dist)
    inner = (1.5 * span - 2.5) * span * span + 1.0
    outer = ((-0.5 * span + 2.5) * span - 4.0) * span + 2.0
    return jnp.where(span < 1.0, inner, jnp.where(span < 2.0, outer, 0.0))


def tap_table(rows, cols, coarse_on_rows, pad):
    r = lax.broadcasted_iota(jnp.float32, (rows, cols), 0)
    c = lax.broadcasted_iota(jnp.float32, (rows, cols), 1)
    if coarse_on_rows:
        coarse, fine = r, c
    else:
        coarse, fine = c, r
    if pad == 4:
        dist = coarse - ((fine - 4.0) * 0.5 + 0.25)
    else:
        dist = coarse - 2.0 - (fine * 0.5 + 0.25)
    return keys_weight(dist).astype(jnp.bfloat16)


def split3(x):
    hi = lax.reduce_precision(x, exponent_bits=8, mantissa_bits=7)
    rest = x - hi
    mid = lax.reduce_precision(rest, exponent_bits=8, mantissa_bits=7)
    lo = rest - mid
    return hi.astype(jnp.bfloat16), mid.astype(jnp.bfloat16), lo.astype(jnp.bfloat16)


def exact_dot(eq, x, table, data_first):
    ins, _ = eq.split("->")
    first, second = ins.split(",")
    if data_first:
        parts = jnp.concatenate(split3(x), axis=first.index(second[0]))
        return jnp.einsum(eq, parts, jnp.concatenate([table] * 3, axis=0), preferred_element_type=jnp.float32)
    parts = jnp.concatenate(split3(x), axis=second.index(first[1]))
    return jnp.einsum(eq, jnp.concatenate([table] * 3, axis=1), parts, preferred_element_type=jnp.float32)


def row_windows(kernel, order, block, width):
    padded = jnp.pad(kernel, ((0, width - kernel.shape[0]), (2, width - block - 2)))
    return jnp.concatenate([padded[:, block * w : block * w + width] for w in order], axis=1)


def body(observed, noise_var, row_kernel, col_kernel):
    highest = lax.Precision.HIGH
    rows_axis = ("yh", "z")
    cols_axis = ("x", "yl", "core")
    tile_rows = row_kernel.shape[0]
    tile_cols = col_kernel.shape[0]
    ext_rows = tile_rows + 8
    row_count = axis_count(rows_axis)
    swap = [(0, 1), (1, 0)]
    side = lax.axis_index("yl")
    span = 4 * tile_cols
    quarters = range(col_kernel.shape[1] // span)
    low = jnp.concatenate([col_kernel[:, q * span : q * span + span // 2] for q in quarters], axis=1)
    high = jnp.concatenate([col_kernel[:, q * span + span // 2 : (q + 1) * span] for q in quarters], axis=1)
    near_cols = jnp.where(side == 0, low, high)
    far_cols = jnp.where(side == 0, high, low)
    partner_cols = lax.ppermute(far_cols, "yl", swap)
    row_rows = with_halo(row_kernel, ((rows_axis, 0),), 2)
    halves_n = axis_count("yh")
    depth = axis_count("z")
    order = [h * depth + d for d in range(depth) for h in range(halves_n)]
    row_big = row_windows(row_rows, order, tile_rows, ext_rows)
    before, after = edges(observed, cols_axis, 2, 4)
    col_adj = tap_table(2 * tile_cols + 8, tile_cols, False, 4)
    row_adj = tap_table(ext_rows, 2 * tile_rows, True, 2)
    colsum = (
        exact_dot("rpq,qj->rpj", observed, col_adj[4:-4], True)
        + exact_dot(
            "rpq,qj->rpj",
            jnp.concatenate([before, after], axis=2),
            jnp.concatenate([col_adj[:4], col_adj[-4:]], axis=0),
            True,
        )
    )
    inducing = exact_dot("ip,rpj->rij", colsum, row_adj, False)
    half = lax.all_gather(inducing, ("x", "core"), axis=2, tiled=True)
    near = jnp.einsum("rik,jk->rij", half, near_cols, precision=highest)
    for_partner = jnp.einsum("rik,jk->rij", half, partner_cols, precision=highest)
    mixed = near + lax.ppermute(for_partner, "yl", swap)
    product = jnp.einsum(
        "ik,rkj->rij", row_big, lax.all_gather(mixed, ("z", "yh"), axis=1, tiled=True), precision=highest
    )
    coarse_ext = with_halo(product, ((cols_axis, 2),), 2)
    row_fwd = tap_table(2 * tile_rows, ext_rows, False, 2)
    col_fwd = tap_table(tile_cols + 4, 2 * tile_cols, True, 2)
    rowpass = exact_dot("pi,rij->rpj", coarse_ext, row_fwd, False)
    result = exact_dot("rpj,jq->rpq", rowpass, col_fwd, True)
    return result + noise_var[None] * observed


def solution(mesh):
    rows_n, cols_n = mesh.devices.shape
    z = min(4, rows_n)
    shape = (rows_n // z, z, cols_n // 4, 2, 2)
    fine = Mesh(mesh.devices.reshape(shape), ("yh", "z", "x", "yl", "core"))
    rows = ("yh", "z")
    cols = ("x", "yl", "core")
    return jax.shard_map(
        body,
        mesh=fine,
        in_specs=(P(None, rows, cols), P(rows, cols), P(rows, None), P(cols, None)),
        out_specs=P(None, rows, cols),
        check_vma=False,
    )
```

```python
import jax
import jax.numpy as jnp
from jax import lax
from jax.sharding import Mesh, PartitionSpec as P


def axis_count(axis):
    return lax.psum(1, axis)


def with_halo(cells, sides, width):
    for axis, dim in sides:
        count = axis_count(axis)
        ends = count - 1
        head = lax.slice_in_dim(cells, 0, width, axis=dim)
        tail = lax.slice_in_dim(cells, cells.shape[dim] - width, cells.shape[dim], axis=dim)
        cells = jnp.concatenate(
            [
                lax.ppermute(tail, axis, [(i, (i + 1) % count) for i in range(ends)]),
                cells,
                lax.ppermute(head, axis, [((i + 1) % count, i) for i in range(ends)]),
            ],
            axis=dim,
        )
    return cells


def edges(cells, axis, dim, width):
    count = axis_count(axis)
    ends = count - 1
    head = lax.slice_in_dim(cells, 0, width, axis=dim)
    tail = lax.slice_in_dim(cells, cells.shape[dim] - width, cells.shape[dim], axis=dim)
    before = lax.ppermute(tail, axis, [(i, i + 1) for i in range(ends)])
    after = lax.ppermute(head, axis, [(i + 1, i) for i in range(ends)])
    return before, after


def keys_weight(dist):
    span = jnp.abs(dist)
    inner = (1.5 * span - 2.5) * span * span + 1.0
    outer = ((-0.5 * span + 2.5) * span - 4.0) * span + 2.0
    return jnp.where(span < 1.0, inner, jnp.where(span < 2.0, outer, 0.0))


def tap_table(rows, cols, coarse_on_rows, pad):
    r = lax.broadcasted_iota(jnp.float32, (rows, cols), 0)
    c = lax.broadcasted_iota(jnp.float32, (rows, cols), 1)
    if coarse_on_rows:
        coarse, fine = r, c
    else:
        coarse, fine = c, r
    if pad == 4:
        dist = coarse - ((fine - 4.0) * 0.5 + 0.25)
    else:
        dist = coarse - 2.0 - (fine * 0.5 + 0.25)
    return keys_weight(dist).astype(jnp.bfloat16)


def split3(x):
    hi = lax.reduce_precision(x, exponent_bits=8, mantissa_bits=7)
    rest = x - hi
    mid = lax.reduce_precision(rest, exponent_bits=8, mantissa_bits=7)
    lo = rest - mid
    return hi.astype(jnp.bfloat16), mid.astype(jnp.bfloat16), lo.astype(jnp.bfloat16)


def exact_dot(eq, x, table, data_first):
    ins, _ = eq.split("->")
    first, second = ins.split(",")
    if data_first:
        parts = jnp.concatenate(split3(x), axis=first.index(second[0]))
        return jnp.einsum(eq, parts, jnp.concatenate([table] * 3, axis=0), preferred_element_type=jnp.float32)
    parts = jnp.concatenate(split3(x), axis=second.index(first[1]))
    return jnp.einsum(eq, jnp.concatenate([table] * 3, axis=1), parts, preferred_element_type=jnp.float32)


def row_windows(kernel, order, block, width):
    padded = jnp.pad(kernel, ((0, width - kernel.shape[0]), (2, width - block - 2)))
    return jnp.concatenate([padded[:, block * w : block * w + width] for w in order], axis=1)


def body(observed, noise_var, row_kernel, col_kernel):
    highest = lax.Precision.HIGH
    rows_axis = ("yh", "z")
    cols_axis = ("x", "yl", "core")
    tile_rows = row_kernel.shape[0]
    tile_cols = col_kernel.shape[0]
    ext_rows = tile_rows + 8
    row_count = axis_count(rows_axis)
    swap = [(0, 1), (1, 0)]
    side = lax.axis_index("yl")
    span = 4 * tile_cols
    quarters = range(col_kernel.shape[1] // span)
    low = jnp.concatenate([col_kernel[:, q * span : q * span + span // 2] for q in quarters], axis=1)
    high = jnp.concatenate([col_kernel[:, q * span + span // 2 : (q + 1) * span] for q in quarters], axis=1)
    near_cols = jnp.where(side == 0, low, high)
    far_cols = jnp.where(side == 0, high, low)
    partner_cols = lax.ppermute(far_cols, "yl", swap)
    row_rows = with_halo(row_kernel, ((rows_axis, 0),), 2)
    halves_n = axis_count("yh")
    depth = axis_count("z")
    order = [h * depth + d for d in range(depth) for h in range(halves_n)]
    row_big = row_windows(row_rows, order, tile_rows, ext_rows)
    before, after = edges(observed, cols_axis, 2, 4)
    col_adj = tap_table(2 * tile_cols + 8, tile_cols, False, 4)
    row_adj = tap_table(ext_rows, 2 * tile_rows, True, 2)
    colsum = (
        exact_dot("rpq,qj->rpj", observed, col_adj[4:-4], True)
        + exact_dot("rpq,qj->rpj", before, col_adj[:4], True)
        + exact_dot("rpq,qj->rpj", after, col_adj[-4:], True)
    )
    inducing = exact_dot("ip,rpj->rij", colsum, row_adj, False)
    half = lax.all_gather(inducing, ("x", "core"), axis=2, tiled=True)
    both = jnp.einsum("rik,jk->rij", half, jnp.concatenate([near_cols, partner_cols], axis=0), precision=highest)
    near = both[..., :tile_cols]
    for_partner = both[..., tile_cols:]
    mixed = near + lax.ppermute(for_partner, "yl", swap)
    product = jnp.einsum(
        "ik,rkj->rij", row_big, lax.all_gather(mixed, ("z", "yh"), axis=1, tiled=True), precision=highest
    )
    coarse_ext = with_halo(product, ((cols_axis, 2),), 2)
    row_fwd = tap_table(2 * tile_rows, ext_rows, False, 2)
    col_fwd = tap_table(tile_cols + 4, 2 * tile_cols, True, 2)
    rowpass = exact_dot("pi,rij->rpj", coarse_ext, row_fwd, False)
    result = exact_dot("rpj,jq->rpq", rowpass, col_fwd, True)
    return result + noise_var[None] * observed


def solution(mesh):
    rows_n, cols_n = mesh.devices.shape
    z = min(4, rows_n)
    shape = (rows_n // z, z, cols_n // 4, 2, 2)
    fine = Mesh(mesh.devices.reshape(shape), ("yh", "z", "x", "yl", "core"))
    rows = ("yh", "z")
    cols = ("x", "yl", "core")
    return jax.shard_map(
        body,
        mesh=fine,
        in_specs=(P(None, rows, cols), P(rows, cols), P(rows, None), P(cols, None)),
        out_specs=P(None, rows, cols),
        check_vma=False,
    )
```
